256 devices in a mesh: ctx: 8 (over z_lo, core), exp: 32 (over y, x, z_hi).
Axes of the slice: x: 4, y: 4, z: 8 (z_hi: 2, z_lo: 4; z = z_hi * 4 + z_lo), core: 2. Of those that a mesh axis runs over, the one named last changes fastest.
Arguments:
- queries: bfloat16 [32, 64, 6144], P('exp', None, 'ctx'), may hold values from -18 to 18
- cached_keys: bfloat16 [32, 1024, 1024], P('exp', 'ctx'), may hold values from -6 to 6
- cached_values: bfloat16 [32, 1024, 1024], P('exp', 'ctx'), may hold values from -6 to 6
- fresh_keys: bfloat16 [32, 64, 1024], P('exp', None, 'ctx'), may hold values from -6 to 6
- fresh_values: bfloat16 [32, 64, 1024], P('exp', None, 'ctx'), may hold values from -6 to 6
- slot_order: int32 [32, 64], P('exp'), may hold values from 0 to 63, each once within a row
- residual: bfloat16 [32, 64, 6144], P('exp'), may hold values from -6 to 6
- expert_ids: int32 [32, 64, 2], P('exp'), may hold values from 0 to 3, all different within a row; in each aligned block of 64 rows (0 to 63, 64 to 127, ..., all dimensions but the last counted through in order) at most 32 rows name the same one
- gate_num: int32 [32, 64, 2], P('exp'), may hold values from 32 to 224, as said below
- gain_attn: float32 [6144], replicated, may hold values from 0.1 to 1.9
- gain_pre: float32 [6144], replicated, may hold values from 0.1 to 1.9
- gain_post: float32 [6144], replicated, may hold values from 0.1 to 1.9
- w_gate: bfloat16 [32, 6144, 2048], P('exp', None, 'ctx'), may hold values from -0.078125 to 0.078125
- w_up: bfloat16 [32, 6144, 2048], P('exp', None, 'ctx'), may hold values from -0.078125 to 0.078125
- w_down: bfloat16 [32, 2048, 6144], P('exp', 'ctx'), may hold values from -0.046875 to 0.046875
Outputs:
- layer_out: bfloat16 [32, 64, 6144], P('exp')
The draws below stay inside these ranges and needn't reach their ends.
Inputs may be any that keep to these rules, and one draw needn't show every extreme that they name: `expert_ids`: each token names 2 different experts; the tokens of one request name each expert exactly 32 times. `gate_num`: the two numbers of a token sum to 256. `slot_order`: within one request the slots of the new tokens are a permutation.
All inputs are finite; a program needn't handle non-finite values.
Results may differ from the reference program's by a relative error of at most 0.012.
Values may be sent and summed in bfloat16 or wider, within the bound.
No kernel may reach another device: no remote copies, remote signals or barrier semaphores. Data moves between devices by JAX's collectives and lax.ppermute only.
A program may use at most 128 MiB of HBM per device.

```python
import math
import jax
import jax.numpy as jnp
import numpy as np
from jax import lax

D = 6144
QUERY_HEADS = 48
KEY_VALUE_HEADS = 8
HEAD_SIZE = 128
EXPERTS = 4
TOP = 2
FF = 16384
NEW_TOKENS = 64
CAP = 32
SPLIT = 8
REQUEST_COUNT = 32
CACHED_TOKENS = 1024
N_CTX = 8
N_EXP = 32


def draw_gate_num(key, part):
    leading = jax.random.randint(key, (REQUEST_COUNT, NEW_TOKENS, 1), 32, 225, dtype=jnp.int32)
    return jnp.concatenate([leading, 256 - leading], axis=-1)


def steps_of(rng, shape, split, least, largest):
    level, own = 1.0, jax.random.fold_in(rng, 6)
    for position, parts in split:
        steps = jnp.exp(jax.random.uniform(jax.random.fold_in(own, position), (parts,), jnp.float32, least / len(split), largest / len(split)))
        level = level * jnp.repeat(steps, shape[position] // parts).reshape([-1 if axis == position else 1 for axis in range(len(shape))])
    return level


def deal_out(rng, own, number, rows, amount, top, reach, skew):
    order = jax.random.permutation(rng, amount)
    packed, common = portions_of(amount, rows * top, reach, skew, True), portions_of(amount, rows * top, reach, skew, False)
    places = jnp.arange(amount)

    def named(lengths, turn):
        used = int((lengths > 0).sum())
        fixed = max(1, used // 4)
        moved = fixed + (places - fixed + turn * (used - fixed)) % max(1, amount - fixed)
        return jnp.zeros((amount,), jnp.int32).at[order[jnp.where(places < fixed, places, moved)]].set(jnp.asarray(lengths, jnp.int32))

    lengths = jnp.where(number % 4 == 0, named(packed, number // 4), named(common, number - number // 4 - 1))
    mixed = jax.random.permutation(jax.random.fold_in(own, 3), amount)
    giver, receiver = mixed[0:amount // 2 * 2:2], mixed[1:amount // 2 * 2:2]
    room = jnp.minimum(lengths[giver] - 1, reach - lengths[receiver]) // 2
    room = jnp.where((giver == order[0]) | (receiver == order[0]) | (lengths[receiver] == 0), 0, jnp.maximum(room, 0))
    moved = jax.random.randint(jax.random.fold_in(own, 4), (amount // 2,), 0, 1 << 20) % (room + 1)
    lengths = lengths.at[giver].add(-moved).at[receiver].add(moved)
    labels = jnp.searchsorted(jnp.cumsum(lengths), jnp.arange(rows * top), side="right").astype(jnp.int32)
    grid = labels.reshape(top, rows).T
    grid = grid[jax.random.permutation(jax.random.fold_in(own, 1), rows)]
    turn = jax.random.randint(jax.random.fold_in(own, 2), (rows, 1), 0, top)
    return jnp.take_along_axis(grid, (jnp.arange(top)[None, :] + turn) % top, axis=1)


def portions_of(count, total, most, slope, full):
    portions = [(1 << 20) // math.isqrt(rank ** slope) + 1 for rank in range(1, count + 1)]
    largest = most if full else min(most, max(-(-total // count), total * portions[0] // sum(portions)))
    least = 1 if total - largest >= count - 1 else 0
    holding, surplus = [largest] + [least] * (count - 1), total - largest - least * (count - 1)
    while surplus > 0:
        candidates = [i for i in range(1, count) if holding[i] < largest] or [i for i in range(1, count) if holding[i] < most]
        pool, left = sum([portions[i] for i in candidates]), surplus
        for i in candidates:
            extra = min(most - holding[i], max(1, left * portions[i] // pool), surplus)
            holding[i] = holding[i] + extra
            surplus = surplus - extra
    return np.array(holding)


def noise(own_key, extent, deviation, bound, pieces=(), kind=jnp.bfloat16):
    entries = jax.random.normal(own_key, extent, jnp.float32) * deviation
    if len(pieces) > 0:
        entries = steps_of(own_key, extent, pieces, -0.22, 0.18) * entries
    return jnp.clip(entries, min=-bound, max=bound).astype(kind)


def setup_inputs(seed: int = 0) -> dict:
    keys = jax.random.split(jax.random.key(seed), 16)
    queries = noise(keys[0], (REQUEST_COUNT, NEW_TOKENS, QUERY_HEADS * HEAD_SIZE), 3.0, 18.0, ((0, 32), (2, 8)))
    cached_keys = noise(keys[1], (REQUEST_COUNT, CACHED_TOKENS, KEY_VALUE_HEADS * HEAD_SIZE), 1.0, 6.0, ((0, 32), (1, 8)))
    cached_values = noise(keys[2], (REQUEST_COUNT, CACHED_TOKENS, KEY_VALUE_HEADS * HEAD_SIZE), 1.0, 6.0, ((0, 32), (1, 8)))
    fresh_keys = noise(keys[3], (REQUEST_COUNT, NEW_TOKENS, KEY_VALUE_HEADS * HEAD_SIZE), 1.0, 6.0, ((0, 32), (2, 8)))
    fresh_values = noise(keys[4], (REQUEST_COUNT, NEW_TOKENS, KEY_VALUE_HEADS * HEAD_SIZE), 1.0, 6.0, ((0, 32), (2, 8)))
    slot_order = jax.vmap(lambda own: jax.random.permutation(own, NEW_TOKENS))(jax.random.split(keys[5], REQUEST_COUNT)).reshape((REQUEST_COUNT, NEW_TOKENS)).astype(jnp.int32)
    residual = noise(keys[6], (REQUEST_COUNT, NEW_TOKENS, D), 1.0, 6.0, ((0, 32),))
    expert_ids_keys = jax.random.split(jax.random.fold_in(keys[7], 1), REQUEST_COUNT * NEW_TOKENS // NEW_TOKENS)
    expert_ids_turns = jax.random.permutation(jax.random.fold_in(keys[7], 3), REQUEST_COUNT * NEW_TOKENS // NEW_TOKENS)
    expert_ids = jax.vmap(lambda own, number: deal_out(jax.random.fold_in(keys[7], 2), own, number, NEW_TOKENS, EXPERTS, TOP, CAP, 0))(expert_ids_keys, expert_ids_turns).reshape((REQUEST_COUNT, NEW_TOKENS, TOP))
    gate_num = draw_gate_num(jax.random.fold_in(keys[15], 71), 0)
    gain_attn = jnp.clip(1.0 + 0.18 * jax.random.normal(keys[9], (D,), jnp.float32), 0.1, 1.9)
    gain_pre = jnp.clip(1.0 + 0.18 * jax.random.normal(keys[10], (D,), jnp.float32), 0.1, 1.9)
    gain_post = jnp.clip(1.0 + 0.18 * jax.random.normal(keys[11], (D,), jnp.float32), 0.1, 1.9)
    w_gate = noise(keys[12], (EXPERTS * SPLIT, D, FF // SPLIT), D ** -0.5, 0.078125, ((0, 32), (2, 8)))
    w_up = noise(keys[13], (EXPERTS * SPLIT, D, FF // SPLIT), D ** -0.5, 0.078125, ((0, 32), (2, 8)))
    w_down = noise(keys[14], (EXPERTS * SPLIT, FF // SPLIT, D), FF ** -0.5, 0.046875, ((0, 32), (1, 8)))
    return {"queries": queries, "cached_keys": cached_keys, "cached_values": cached_values, "fresh_keys": fresh_keys, "fresh_values": fresh_values, "slot_order": slot_order, "residual": residual, "expert_ids": expert_ids, "gate_num": gate_num, "gain_attn": gain_attn, "gain_pre": gain_pre, "gain_post": gain_post, "w_gate": w_gate, "w_up": w_up, "w_down": w_down}


def normalize(values, scaling):
    return values * lax.rsqrt(lax.optimization_barrier(jnp.mean(values * values, axis=-1, keepdims=True)) + 1e-05) * scaling

def route_tables(expert_ids, gate_num):
    blocks = expert_ids.shape[0]
    per_block = expert_ids.shape[1]
    top_k = expert_ids.shape[2]
    flat_ids = expert_ids.reshape(blocks, per_block * top_k).astype(jnp.int32)
    onehot = (flat_ids[..., None] == jnp.arange(EXPERTS, dtype=jnp.int32)).astype(jnp.int32)
    before = jnp.cumsum(onehot, axis=1) - onehot
    slot_num = lax.optimization_barrier(jnp.sum(onehot * before, axis=-1))
    target = flat_ids * CAP + slot_num
    one_table = (target[..., None] == jnp.arange(EXPERTS * CAP, dtype=jnp.int32)).astype(jnp.float32)
    one_table = one_table.reshape(blocks, per_block, top_k, EXPERTS * CAP)
    fractions = gate_num.astype(jnp.float32) / 256.0
    dispatch = lax.optimization_barrier(jnp.sum(one_table, axis=2))
    combine = lax.optimization_barrier(jnp.sum(one_table * fractions[..., None], axis=2))
    return (dispatch, combine)

def attend_one(query_row_block, query_slot, key_row_block, value_row_block, key_slot):
    query_count = query_row_block.shape[0]
    key_count = key_row_block.shape[0]
    query_groups = QUERY_HEADS // KEY_VALUE_HEADS
    query_head_rows = query_row_block.astype(jnp.float32).reshape(query_count, KEY_VALUE_HEADS, query_groups, HEAD_SIZE)
    key_head_rows = key_row_block.astype(jnp.float32).reshape(key_count, KEY_VALUE_HEADS, HEAD_SIZE)
    value_head_rows = value_row_block.astype(jnp.float32).reshape(key_count, KEY_VALUE_HEADS, HEAD_SIZE)
    scores = jnp.einsum('qhgd,khd->hgqk', query_head_rows, key_head_rows) * HEAD_SIZE ** (-0.5)
    capped = 30.0 * jnp.tanh(scores / 30.0)
    visible = key_slot[None, None, None, :] <= query_slot[None, None, :, None]
    attn_weights = jnp.where(visible, jnp.exp(capped), 0.0)
    attn_weights = lax.optimization_barrier(attn_weights.astype(jnp.bfloat16)).astype(jnp.float32)
    totals = lax.optimization_barrier(jnp.sum(attn_weights, axis=-1))
    numerator = jnp.einsum('hgqk,khd->qhgd', attn_weights, value_head_rows)
    attended = numerator / jnp.transpose(totals, (2, 0, 1))[..., None]
    return attended.reshape(query_count, QUERY_HEADS * HEAD_SIZE)

def reference(queries, cached_keys, cached_values, fresh_keys, fresh_values, slot_order, residual, expert_ids, gate_num, gain_attn, gain_pre, gain_post, w_gate, w_up, w_down):

    def per_request(items):
        q_rows, k_old, v_old, k_fresh, v_fresh, slots = items
        key_row_block = jnp.concatenate([k_old, k_fresh], axis=0)
        value_row_block = jnp.concatenate([v_old, v_fresh], axis=0)
        key_slot = jnp.concatenate([jnp.full((k_old.shape[0],), -1, jnp.int32), slots.astype(jnp.int32)])
        return attend_one(q_rows, slots.astype(jnp.int32), key_row_block, value_row_block, key_slot)
    attended = lax.map(per_request, (queries, cached_keys, cached_values, fresh_keys, fresh_values, slot_order))
    hidden_state = (residual.astype(jnp.float32) + normalize(attended, gain_attn)).astype(jnp.bfloat16)
    normed = normalize(hidden_state.astype(jnp.float32), gain_pre).astype(jnp.bfloat16)
    n_blocks = REQUEST_COUNT
    dispatch, combine = route_tables(expert_ids, gate_num)
    buffers = jnp.einsum('bns,bnd->bsd', dispatch, normed.astype(jnp.float32)).astype(jnp.bfloat16)
    expert_rows = jnp.transpose(buffers.reshape(n_blocks, EXPERTS, CAP, D), (1, 0, 2, 3)).reshape(EXPERTS, n_blocks * CAP, D)
    split_count = N_EXP // EXPERTS
    gate_all = w_gate.reshape(EXPERTS, split_count, D, FF // split_count)
    up_all = w_up.reshape(EXPERTS, split_count, D, FF // split_count)
    down_all = w_down.reshape(EXPERTS, split_count, FF // split_count, D)

    def per_expert(items):
        row_block, gate_set, up_set, down_set = items

        def per_split(running, matrices):
            gate_mat, up_mat, down_mat = matrices
            pre_gate = jnp.dot(row_block, gate_mat, preferred_element_type=jnp.float32)
            pre_up = jnp.dot(row_block, up_mat, preferred_element_type=jnp.float32)
            hidden_units = (jax.nn.gelu(pre_gate) * pre_up).astype(jnp.bfloat16)
            hid_parts = lax.optimization_barrier(hidden_units).astype(jnp.float32).reshape(row_block.shape[0], N_CTX, -1)
            down_parts = down_mat.astype(jnp.float32).reshape(N_CTX, -1, D)
            partial_value = jnp.einsum('rch,chd->crd', hid_parts, down_parts)
            partial_value = lax.optimization_barrier(partial_value.astype(jnp.bfloat16)).astype(jnp.float32)
            return (running + lax.optimization_barrier(jnp.sum(partial_value, axis=0)), None)
        start_rows = jnp.zeros((row_block.shape[0], D), jnp.float32)
        return lax.scan(per_split, start_rows, (gate_set, up_set, down_set))[0]
    outputs = lax.map(per_expert, (expert_rows, gate_all, up_all, down_all))
    gathered = jnp.transpose(outputs.reshape(EXPERTS, n_blocks, CAP, D), (1, 0, 2, 3)).reshape(n_blocks, EXPERTS * CAP, D)
    mixture = jnp.einsum('bns,bsd->bnd', combine, gathered, precision=lax.Precision.HIGHEST)
    result = hidden_state.astype(jnp.float32) + normalize(mixture, gain_post)
    return result.astype(jnp.bfloat16)
```

```python
import jax
import jax.numpy as jnp
import numpy as np
from jax import lax
from jax.sharding import Mesh
from jax.sharding import PartitionSpec as P

D = 6144
HEAD_SIZE = 128
EXPERTS = 4
CAP = 32
EPS = 1e-05

CTX = ("zl", "core")
REQ = ("y", "x", "zh")


def route_tables(expert_ids, gate_num):
    blocks = expert_ids.shape[0]
    per_block = expert_ids.shape[1]
    top_k = expert_ids.shape[2]
    flat_ids = expert_ids.reshape(blocks, per_block * top_k)
    onehot = (flat_ids[..., None] == jnp.arange(EXPERTS, dtype=jnp.int32)).astype(jnp.int32)
    before = jnp.cumsum(onehot, axis=1) - onehot
    slot_num = jnp.sum(onehot * before, axis=-1)
    target = flat_ids * CAP + slot_num
    one_table = (target[..., None] == jnp.arange(EXPERTS * CAP, dtype=jnp.int32)).astype(
        jnp.float32
    )
    one_table = one_table.reshape(blocks, per_block, top_k, EXPERTS * CAP)
    fractions = gate_num.astype(jnp.float32) / 256.0
    dispatch = jnp.sum(one_table, axis=2)
    combine = jnp.sum(one_table * fractions[..., None], axis=2)
    return (dispatch, combine)


def attend_part(query_row_block, query_slot, key_row_block, value_row_block, key_slot):
    query_count = query_row_block.shape[0]
    key_count = key_row_block.shape[0]
    n_kv = key_row_block.shape[1] // HEAD_SIZE
    query_groups = query_row_block.shape[1] // HEAD_SIZE // n_kv
    query_head_rows = query_row_block.reshape(query_count, n_kv, query_groups, HEAD_SIZE)
    key_head_rows = key_row_block.reshape(key_count, n_kv, HEAD_SIZE)
    value_head_rows = value_row_block.reshape(key_count, n_kv, HEAD_SIZE)
    scores = jnp.einsum(
        "qhgd,khd->hgqk", query_head_rows, key_head_rows, preferred_element_type=jnp.float32
    ) * HEAD_SIZE ** (-0.5)
    capped = 30.0 * jnp.tanh(scores / 30.0)
    visible = key_slot[None, None, None, :] <= query_slot[None, None, :, None]
    attn_weights = jnp.where(visible, jnp.exp(capped), 0.0).astype(jnp.bfloat16)
    totals = jnp.sum(attn_weights.astype(jnp.float32), axis=-1)
    totals = jnp.transpose(totals, (2, 0, 1)).reshape(query_count, n_kv * query_groups)
    numerator = jnp.einsum(
        "hgqk,khd->qhgd", attn_weights, value_head_rows, preferred_element_type=jnp.float32
    )
    return (numerator.reshape(query_count, n_kv * query_groups * HEAD_SIZE), totals)


def col_slice(values, width):
    start = lax.axis_index(CTX) * width
    return lax.dynamic_slice_in_dim(values, start, width, values.ndim - 1)


def row_scale(local_rows, gain_cols):
    sum_sq = lax.psum(jnp.sum(local_rows * local_rows, axis=-1, keepdims=True), CTX)
    return local_rows * lax.rsqrt(sum_sq / D + EPS) * gain_cols


def per_device(
    queries,
    cached_keys,
    cached_values,
    fresh_keys,
    fresh_values,
    slot_order,
    residual,
    expert_ids,
    gate_num,
    gain_attn,
    gain_pre,
    gain_post,
    w_gate,
    w_up,
    w_down,
):
    query_row_block = queries[0]
    query_count = query_row_block.shape[0]
    width = query_row_block.shape[1]
    query_slot = slot_order[0].astype(jnp.float32)
    head_width = fresh_keys.shape[2]
    n_ctx = D // width

    with jax.named_scope("attention"):
        new_numer, new_totals = attend_part(
            query_row_block, query_slot, fresh_keys[0], fresh_values[0], query_slot
        )
        cache_rows = cached_keys.shape[1]
        key_heads = cached_keys[0].reshape(cache_rows, n_ctx, head_width)
        value_heads = cached_values[0].reshape(cache_rows, n_ctx, head_width)
        key_part = lax.all_to_all(key_heads, CTX, split_axis=1, concat_axis=0, tiled=True)
        value_part = lax.all_to_all(value_heads, CTX, split_axis=1, concat_axis=0, tiled=True)
        key_part = key_part.reshape(-1, head_width)
        value_part = value_part.reshape(-1, head_width)
        cache_slot = jnp.full((key_part.shape[0],), -1.0, jnp.float32)
        numer_part, total_part = attend_part(
            query_row_block, query_slot, key_part, value_part, cache_slot
        )
        numerator = new_numer + numer_part
        totals = new_totals + total_part
        local_heads = (
            numerator.reshape(query_count, -1, HEAD_SIZE) / totals[..., None]
        ).reshape(query_count, -1)

    with jax.named_scope("norms"):
        residual_cols = col_slice(residual[0], width).astype(jnp.float32)
        hidden_cols = (residual_cols + row_scale(local_heads, col_slice(gain_attn, width))).astype(
            jnp.bfloat16
        )
        normed_cols = row_scale(hidden_cols.astype(jnp.float32), col_slice(gain_pre, width)).astype(
            jnp.bfloat16
        )

    dispatch, combine = route_tables(expert_ids, gate_num)
    with jax.named_scope("dispatch"):
        buffer = jnp.einsum(
            "ns,nd->sd",
            dispatch[0].astype(jnp.bfloat16),
            normed_cols,
            preferred_element_type=jnp.float32,
        ).astype(jnp.bfloat16)
        rows = buffer.reshape(EXPERTS, CAP, width)
        rows = lax.all_to_all(rows, "y", split_axis=0, concat_axis=0, tiled=True)
        rows = lax.all_gather(rows, ("zh", "zl"), axis=0, tiled=False)
        rows = lax.all_gather(rows, "x", axis=0, tiled=False)
        rows = lax.all_gather(rows, "core", axis=0, tiled=False)
        n_core, n_x, n_z, n_y = rows.shape[:4]
        n_zh = 2
        n_zl = n_z // n_zh
        rows = rows.reshape(n_core, n_x, n_zh, n_zl, n_y, CAP, width)
        flat_rows = jnp.transpose(rows, (1, 2, 4, 5, 3, 0, 6)).reshape(
            n_x * n_zh * n_y * CAP, D
        )

    with jax.named_scope("experts"):
        pre_gate = jnp.dot(flat_rows, w_gate[0], preferred_element_type=jnp.float32)
        pre_up = jnp.dot(flat_rows, w_up[0], preferred_element_type=jnp.float32)
        hidden_units = (jax.nn.gelu(pre_gate) * pre_up).astype(jnp.bfloat16)
        projected = jnp.dot(hidden_units, w_down[0], preferred_element_type=jnp.float32).astype(
            jnp.bfloat16
        )

    with jax.named_scope("combine"):
        parts = projected.reshape(n_x, n_zh, n_y, CAP, n_zl, n_core, width)
        parts = jnp.transpose(parts, (5, 0, 1, 4, 2, 3, 6))
        parts = lax.psum_scatter(parts, "core", scatter_dimension=0, tiled=False)
        parts = lax.psum_scatter(parts, "x", scatter_dimension=0, tiled=False)
        parts = lax.psum_scatter(
            parts.reshape(n_zh * n_zl, n_y, CAP, width), ("zh", "zl"), scatter_dimension=0, tiled=False
        )
        outs = lax.all_to_all(parts, "y", split_axis=0, concat_axis=0, tiled=True)
        expert_cols = outs.reshape(EXPERTS * CAP, width).astype(jnp.float32)
        mixture = jnp.dot(combine[0], expert_cols, precision=lax.Precision.HIGHEST)
        layer_cols = (
            hidden_cols.astype(jnp.float32) + row_scale(mixture, col_slice(gain_post, width))
        ).astype(jnp.bfloat16)
        layer_out = lax.all_gather(layer_cols, CTX, axis=1, tiled=True)
    return layer_out[None]


def solution(mesh):
    n_exp = mesh.shape["exp"]
    n_ctx = mesh.shape["ctx"]
    sizes = {"y": EXPERTS, "x": n_exp // EXPERTS // 2, "zh": 2, "zl": n_ctx // 2, "core": 2}
    parts = {"exp": ("y", "x", "zh"), "ctx": ("zl", "core")}
    names = tuple(n for axis in mesh.axis_names for n in parts[axis])
    devices = np.asarray(mesh.devices).reshape(tuple(sizes[n] for n in names))
    fine = Mesh(devices, names)
    in_specs = (
        P(REQ, None, CTX),
        P(REQ, CTX, None),
        P(REQ, CTX, None),
        P(REQ, None, CTX),
        P(REQ, None, CTX),
        P(REQ, None),
        P(REQ, None, None),
        P(REQ, None, None),
        P(REQ, None, None),
        P(),
        P(),
        P(),
        P(REQ, None, CTX),
        P(REQ, None, CTX),
        P(REQ, CTX, None),
    )
    out_specs = P(REQ, None, None)
    return jax.shard_map(
        per_device, mesh=fine, in_specs=in_specs, out_specs=out_specs, check_vma=False
    )
```

```python
import jax
import jax.numpy as jnp
import numpy as np
from jax import lax
from jax.sharding import Mesh
from jax.sharding import PartitionSpec as P

D = 6144
HEAD_SIZE = 128
EXPERTS = 4
CAP = 32
EPS = 1e-05

CTX = ("zl", "core")
REQ = ("y", "x", "zh")


def route_tables(expert_ids, gate_num):
    blocks = expert_ids.shape[0]
    per_block = expert_ids.shape[1]
    top_k = expert_ids.shape[2]
    flat_ids = expert_ids.reshape(blocks, per_block * top_k)
    onehot = (flat_ids[..., None] == jnp.arange(EXPERTS, dtype=jnp.int32)).astype(jnp.int32)
    before = jnp.cumsum(onehot, axis=1) - onehot
    slot_num = jnp.sum(onehot * before, axis=-1)
    target = flat_ids * CAP + slot_num
    one_table = (target[..., None] == jnp.arange(EXPERTS * CAP, dtype=jnp.int32)).astype(
        jnp.float32
    )
    one_table = one_table.reshape(blocks, per_block, top_k, EXPERTS * CAP)
    fractions = gate_num.astype(jnp.float32) / 256.0
    dispatch = jnp.sum(one_table, axis=2)
    combine = jnp.sum(one_table * fractions[..., None], axis=2)
    return (dispatch, combine)


def attend_part(query_row_block, query_slot, key_row_block, value_row_block, key_slot):
    query_count = query_row_block.shape[0]
    key_count = key_row_block.shape[0]
    n_kv = key_row_block.shape[1] // HEAD_SIZE
    query_groups = query_row_block.shape[1] // HEAD_SIZE // n_kv
    query_head_rows = query_row_block.reshape(query_count, n_kv, query_groups, HEAD_SIZE)
    key_head_rows = key_row_block.reshape(key_count, n_kv, HEAD_SIZE)
    value_head_rows = value_row_block.reshape(key_count, n_kv, HEAD_SIZE)
    scores = jnp.einsum(
        "qhgd,khd->hgqk", query_head_rows, key_head_rows, preferred_element_type=jnp.float32
    ) * HEAD_SIZE ** (-0.5)
    capped = 30.0 * jnp.tanh(scores / 30.0)
    visible = key_slot[None, None, None, :] <= query_slot[None, None, :, None]
    attn_weights = jnp.where(visible, jnp.exp(capped), 0.0).astype(jnp.bfloat16)
    totals = jnp.sum(attn_weights.astype(jnp.float32), axis=-1)
    totals = jnp.transpose(totals, (2, 0, 1)).reshape(query_count, n_kv * query_groups)
    numerator = jnp.einsum(
        "hgqk,khd->qhgd", attn_weights, value_head_rows, preferred_element_type=jnp.float32
    )
    return (numerator.reshape(query_count, n_kv * query_groups * HEAD_SIZE), totals)


def col_slice(values, width):
    start = lax.axis_index(CTX) * width
    return lax.dynamic_slice_in_dim(values, start, width, values.ndim - 1)


def row_scale(local_rows, gain_cols):
    sum_sq = lax.psum(jnp.sum(local_rows * local_rows, axis=-1, keepdims=True), CTX)
    return local_rows * lax.rsqrt(sum_sq / D + EPS) * gain_cols


def per_device(
    queries,
    cached_keys,
    cached_values,
    fresh_keys,
    fresh_values,
    slot_order,
    residual,
    expert_ids,
    gate_num,
    gain_attn,
    gain_pre,
    gain_post,
    w_gate,
    w_up,
    w_down,
):
    query_row_block = queries[0]
    query_count = query_row_block.shape[0]
    width = query_row_block.shape[1]
    query_slot = slot_order[0].astype(jnp.float32)
    head_width = fresh_keys.shape[2]
    n_ctx = D // width

    with jax.named_scope("attention"):
        new_numer, new_totals = attend_part(
            query_row_block, query_slot, fresh_keys[0], fresh_values[0], query_slot
        )
        cache_rows = cached_keys.shape[1]
        key_heads = cached_keys[0].reshape(cache_rows, n_ctx, head_width)
        value_heads = cached_values[0].reshape(cache_rows, n_ctx, head_width)
        key_part = lax.all_to_all(key_heads, CTX, split_axis=1, concat_axis=0, tiled=True)
        value_part = lax.all_to_all(value_heads, CTX, split_axis=1, concat_axis=0, tiled=True)
        key_part = key_part.reshape(-1, head_width)
        value_part = value_part.reshape(-1, head_width)
        cache_slot = jnp.full((key_part.shape[0],), -1.0, jnp.float32)
        numer_part, total_part = attend_part(
            query_row_block, query_slot, key_part, value_part, cache_slot
        )
        numerator = new_numer + numer_part
        totals = new_totals + total_part
        local_heads = (
            numerator.reshape(query_count, -1, HEAD_SIZE) / totals[..., None]
        ).reshape(query_count, -1)

    with jax.named_scope("norms"):
        residual_cols = col_slice(residual[0], width).astype(jnp.float32)
        hidden_cols = (residual_cols + row_scale(local_heads, col_slice(gain_attn, width))).astype(
            jnp.bfloat16
        )
        normed_cols = row_scale(hidden_cols.astype(jnp.float32), col_slice(gain_pre, width)).astype(
            jnp.bfloat16
        )

    dispatch, combine = route_tables(expert_ids, gate_num)
    n_zl = D // width // 2
    group = CAP // n_zl
    swap = [(0, 1), (1, 0)]
    with jax.named_scope("dispatch"):
        buffer = jnp.einsum(
            "ns,nd->sd",
            dispatch[0].astype(jnp.bfloat16),
            normed_cols,
            preferred_element_type=jnp.float32,
        ).astype(jnp.bfloat16)
        rows = buffer.reshape(EXPERTS, n_zl, group, 1, width)
        rows = lax.all_to_all(rows, "zl", split_axis=1, concat_axis=3, tiled=True)
        rows = rows.reshape(EXPERTS, group, n_zl, width)
        rows = lax.all_to_all(rows, "y", split_axis=0, concat_axis=0, tiled=True)
        rows = lax.all_gather(rows, ("zh", "zl"), axis=0, tiled=True)
        rows = lax.all_gather(rows, "x", axis=0, tiled=True)
        own_rows = rows.reshape(-1, n_zl * width)
        other_rows = lax.ppermute(own_rows, "core", swap)

    with jax.named_scope("experts"):
        core = lax.axis_index("core")

        def halves(mat, axis):
            shape = mat.shape
            split = shape[:axis] + (n_zl, 2, width) + shape[axis + 1 :]
            mat = mat.reshape(split)
            own = lax.dynamic_index_in_dim(mat, core, axis + 1, keepdims=False)
            other = lax.dynamic_index_in_dim(mat, 1 - core, axis + 1, keepdims=False)
            merged = shape[:axis] + (n_zl * width,) + shape[axis + 1 :]
            return own.reshape(merged), other.reshape(merged)

        gate_own, gate_other = halves(w_gate[0], 0)
        up_own, up_other = halves(w_up[0], 0)
        down_own, down_other = halves(w_down[0], 1)
        pre_gate = jnp.dot(own_rows, gate_own, preferred_element_type=jnp.float32) + jnp.dot(
            other_rows, gate_other, preferred_element_type=jnp.float32
        )
        pre_up = jnp.dot(own_rows, up_own, preferred_element_type=jnp.float32) + jnp.dot(
            other_rows, up_other, preferred_element_type=jnp.float32
        )
        hidden_units = (jax.nn.gelu(pre_gate) * pre_up).astype(jnp.bfloat16)
        piece_own = jnp.dot(hidden_units, down_own, preferred_element_type=jnp.float32).astype(
            jnp.bfloat16
        )
        piece_other = jnp.dot(
            hidden_units, down_other, preferred_element_type=jnp.float32
        ).astype(jnp.bfloat16)

    with jax.named_scope("combine"):
        received = lax.ppermute(piece_other, "core", swap)
        parts = (piece_own.astype(jnp.float32) + received.astype(jnp.float32)).astype(jnp.bfloat16)
        parts = parts.reshape(rows.shape)
        parts = lax.psum_scatter(parts, "x", scatter_dimension=0, tiled=True)
        parts = parts.reshape((2 * n_zl, -1) + parts.shape[1:])
        parts = lax.psum_scatter(parts, ("zh", "zl"), scatter_dimension=0, tiled=False)
        outs = lax.all_to_all(parts, "y", split_axis=0, concat_axis=0, tiled=True)
        outs = outs.reshape(EXPERTS, 1, group, n_zl, width)
        outs = lax.all_to_all(outs, "zl", split_axis=3, concat_axis=1, tiled=True)
        expert_cols = outs.reshape(EXPERTS * CAP, width).astype(jnp.float32)
        mixture = jnp.dot(combine[0], expert_cols, precision=lax.Precision.HIGHEST)
        layer_cols = (
            hidden_cols.astype(jnp.float32) + row_scale(mixture, col_slice(gain_post, width))
        ).astype(jnp.bfloat16)
        layer_out = lax.all_gather(layer_cols, CTX, axis=1, tiled=True)
    return layer_out[None]


def solution(mesh):
    n_exp = mesh.shape["exp"]
    n_ctx = mesh.shape["ctx"]
    sizes = {"y": EXPERTS, "x": n_exp // EXPERTS // 2, "zh": 2, "zl": n_ctx // 2, "core": 2}
    parts = {"exp": ("y", "x", "zh"), "ctx": ("zl", "core")}
    names = tuple(n for axis in mesh.axis_names for n in parts[axis])
    devices = np.asarray(mesh.devices).reshape(tuple(sizes[n] for n in names))
    fine = Mesh(devices, names)
    in_specs = (
        P(REQ, None, CTX),
        P(REQ, CTX, None),
        P(REQ, CTX, None),
        P(REQ, None, CTX),
        P(REQ, None, CTX),
        P(REQ, None),
        P(REQ, None, None),
        P(REQ, None, None),
        P(REQ, None, None),
        P(),
        P(),
        P(),
        P(REQ, None, CTX),
        P(REQ, None, CTX),
        P(REQ, CTX, None),
    )
    out_specs = P(REQ, None, None)
    return jax.shard_map(
        per_device, mesh=fine, in_specs=in_specs, out_specs=out_specs, check_vma=False
    )
```

```python
import jax
import jax.numpy as jnp
import numpy as np
from jax import lax
from jax.sharding import Mesh
from jax.sharding import PartitionSpec as P

D = 6144
HEAD_SIZE = 128
EXPERTS = 4
CAP = 32
EPS = 1e-05

CTX = ("zl", "core")
REQ = ("y", "x", "zh")


def route_tables(expert_ids, gate_num):
    blocks = expert_ids.shape[0]
    per_block = expert_ids.shape[1]
    top_k = expert_ids.shape[2]
    flat_ids = expert_ids.reshape(blocks, per_block * top_k)
    onehot = (flat_ids[..., None] == jnp.arange(EXPERTS, dtype=jnp.int32)).astype(jnp.int32)
    before = jnp.cumsum(onehot, axis=1) - onehot
    slot_num = jnp.sum(onehot * before, axis=-1)
    target = flat_ids * CAP + slot_num
    one_table = (target[..., None] == jnp.arange(EXPERTS * CAP, dtype=jnp.int32)).astype(
        jnp.float32
    )
    one_table = one_table.reshape(blocks, per_block, top_k, EXPERTS * CAP)
    fractions = gate_num.astype(jnp.float32) / 256.0
    dispatch = jnp.sum(one_table, axis=2)
    combine = jnp.sum(one_table * fractions[..., None], axis=2)
    return (dispatch, combine)


def attend_part(query_row_block, query_slot, key_row_block, value_row_block, key_slot):
    query_count = query_row_block.shape[0]
    key_count = key_row_block.shape[0]
    n_kv = key_row_block.shape[1] // HEAD_SIZE
    query_groups = query_row_block.shape[1] // HEAD_SIZE // n_kv
    query_head_rows = query_row_block.reshape(query_count, n_kv, query_groups, HEAD_SIZE)
    key_head_rows = key_row_block.reshape(key_count, n_kv, HEAD_SIZE)
    value_head_rows = value_row_block.reshape(key_count, n_kv, HEAD_SIZE)
    scores = jnp.einsum(
        "qhgd,khd->hgqk", query_head_rows, key_head_rows, preferred_element_type=jnp.float32
    ) * HEAD_SIZE ** (-0.5)
    capped = 30.0 * jnp.tanh(scores / 30.0)
    visible = key_slot[None, None, None, :] <= query_slot[None, None, :, None]
    attn_weights = jnp.where(visible, jnp.exp(capped), 0.0).astype(jnp.bfloat16)
    totals = jnp.sum(attn_weights.astype(jnp.float32), axis=-1)
    totals = jnp.transpose(totals, (2, 0, 1)).reshape(query_count, n_kv * query_groups)
    numerator = jnp.einsum(
        "hgqk,khd->qhgd", attn_weights, value_head_rows, preferred_element_type=jnp.float32
    )
    return (numerator.reshape(query_count, n_kv * query_groups * HEAD_SIZE), totals)


def col_slice(values, width):
    start = lax.axis_index(CTX) * width
    return lax.dynamic_slice_in_dim(values, start, width, values.ndim - 1)


def row_scale(local_rows, gain_cols):
    sum_sq = lax.psum(jnp.sum(local_rows * local_rows, axis=-1, keepdims=True), CTX)
    return local_rows * lax.rsqrt(sum_sq / D + EPS) * gain_cols


def per_device(
    queries,
    cached_keys,
    cached_values,
    fresh_keys,
    fresh_values,
    slot_order,
    residual,
    expert_ids,
    gate_num,
    gain_attn,
    gain_pre,
    gain_post,
    w_gate,
    w_up,
    w_down,
):
    query_row_block = queries[0]
    query_count = query_row_block.shape[0]
    width = query_row_block.shape[1]
    query_slot = slot_order[0].astype(jnp.float32)
    head_width = fresh_keys.shape[2]
    n_ctx = D // width

    with jax.named_scope("attention"):
        new_numer, new_totals = attend_part(
            query_row_block, query_slot, fresh_keys[0], fresh_values[0], query_slot
        )
        cache_rows = cached_keys.shape[1]
        both_heads = jnp.stack([cached_keys[0], cached_values[0]]).reshape(
            2, cache_rows, n_ctx, head_width
        )
        both_part = lax.all_to_all(both_heads, CTX, split_axis=2, concat_axis=1, tiled=True)
        key_part = both_part[0].reshape(-1, head_width)
        value_part = both_part[1].reshape(-1, head_width)
        cache_slot = jnp.full((key_part.shape[0],), -1.0, jnp.float32)
        numer_part, total_part = attend_part(
            query_row_block, query_slot, key_part, value_part, cache_slot
        )
        numerator = new_numer + numer_part
        totals = new_totals + total_part
        local_heads = (
            numerator.reshape(query_count, -1, HEAD_SIZE) / totals[..., None]
        ).reshape(query_count, -1)

    with jax.named_scope("norms"):
        residual_cols = col_slice(residual[0], width).astype(jnp.float32)
        hidden_cols = (residual_cols + row_scale(local_heads, col_slice(gain_attn, width))).astype(
            jnp.bfloat16
        )
        normed_cols = row_scale(hidden_cols.astype(jnp.float32), col_slice(gain_pre, width)).astype(
            jnp.bfloat16
        )

    dispatch, combine = route_tables(expert_ids, gate_num)
    n_zl = D // width // 2
    group = CAP // n_zl
    swap = [(0, 1), (1, 0)]
    with jax.named_scope("dispatch"):
        buffer = jnp.einsum(
            "ns,nd->sd",
            dispatch[0].astype(jnp.bfloat16),
            normed_cols,
            preferred_element_type=jnp.float32,
        ).astype(jnp.bfloat16)
        rows = buffer.reshape(EXPERTS * n_zl, group, width)
        rows = lax.all_to_all(rows, ("y", "zl"), split_axis=0, concat_axis=0, tiled=True)
        rows = jnp.transpose(rows.reshape(EXPERTS, n_zl, group, width), (0, 2, 1, 3))
        rows = lax.all_gather(rows, ("zh", "zl"), axis=0, tiled=True)
        rows = lax.all_gather(rows, "x", axis=0, tiled=True)
        own_rows = rows.reshape(-1, n_zl * width)
        other_rows = lax.ppermute(own_rows, "core", swap)

    with jax.named_scope("experts"):
        core = lax.axis_index("core")

        def halves(mat, axis):
            shape = mat.shape
            split = shape[:axis] + (n_zl, 2, width) + shape[axis + 1 :]
            mat = mat.reshape(split)
            own = lax.dynamic_index_in_dim(mat, core, axis + 1, keepdims=False)
            other = lax.dynamic_index_in_dim(mat, 1 - core, axis + 1, keepdims=False)
            merged = shape[:axis] + (n_zl * width,) + shape[axis + 1 :]
            return own.reshape(merged), other.reshape(merged)

        gate_own, gate_other = halves(w_gate[0], 0)
        up_own, up_other = halves(w_up[0], 0)
        down_own, down_other = halves(w_down[0], 1)
        pre_gate = jnp.dot(own_rows, gate_own, preferred_element_type=jnp.float32) + jnp.dot(
            other_rows, gate_other, preferred_element_type=jnp.float32
        )
        pre_up = jnp.dot(own_rows, up_own, preferred_element_type=jnp.float32) + jnp.dot(
            other_rows, up_other, preferred_element_type=jnp.float32
        )
        hidden_units = (jax.nn.gelu(pre_gate) * pre_up).astype(jnp.bfloat16)
        piece_own = jnp.dot(hidden_units, down_own, preferred_element_type=jnp.float32).astype(
            jnp.bfloat16
        )
        piece_other = jnp.dot(
            hidden_units, down_other, preferred_element_type=jnp.float32
        ).astype(jnp.bfloat16)

    with jax.named_scope("combine"):
        received = lax.ppermute(piece_other, "core", swap)
        parts = (piece_own.astype(jnp.float32) + received.astype(jnp.float32)).astype(jnp.bfloat16)
        parts = parts.reshape(rows.shape)
        parts = lax.psum_scatter(parts, "x", scatter_dimension=0, tiled=True)
        parts = parts.reshape((2 * n_zl, -1) + parts.shape[1:])
        parts = lax.psum_scatter(parts, ("zh", "zl"), scatter_dimension=0, tiled=False)
        parts = jnp.transpose(parts.reshape(EXPERTS, group, n_zl, width), (0, 2, 1, 3))
        parts = parts.reshape(EXPERTS * n_zl, group, width)
        outs = lax.all_to_all(parts, ("y", "zl"), split_axis=0, concat_axis=0, tiled=True)
        expert_cols = outs.reshape(EXPERTS * CAP, width).astype(jnp.float32)
        mixture = jnp.dot(combine[0], expert_cols, precision=lax.Precision.HIGHEST)
        layer_cols = (
            hidden_cols.astype(jnp.float32) + row_scale(mixture, col_slice(gain_post, width))
        ).astype(jnp.bfloat16)
        layer_out = lax.all_gather(layer_cols, CTX, axis=1, tiled=True)
    return layer_out[None]


def solution(mesh):
    n_exp = mesh.shape["exp"]
    n_ctx = mesh.shape["ctx"]
    sizes = {"y": EXPERTS, "x": n_exp // EXPERTS // 2, "zh": 2, "zl": n_ctx // 2, "core": 2}
    parts = {"exp": ("y", "x", "zh"), "ctx": ("zl", "core")}
    names = tuple(n for axis in mesh.axis_names for n in parts[axis])
    devices = np.asarray(mesh.devices).reshape(tuple(sizes[n] for n in names))
    fine = Mesh(devices, names)
    in_specs = (
        P(REQ, None, CTX),
        P(REQ, CTX, None),
        P(REQ, CTX, None),
        P(REQ, None, CTX),
        P(REQ, None, CTX),
        P(REQ, None),
        P(REQ, None, None),
        P(REQ, None, None),
        P(REQ, None, None),
        P(),
        P(),
        P(),
        P(REQ, None, CTX),
        P(REQ, None, CTX),
        P(REQ, CTX, None),
    )
    out_specs = P(REQ, None, None)
    return jax.shard_map(
        per_device, mesh=fine, in_specs=in_specs, out_specs=out_specs, check_vma=False
    )
```

```python
import jax
import jax.numpy as jnp
import numpy as np
from jax import lax
from jax.sharding import Mesh
from jax.sharding import PartitionSpec as P

D = 6144
HEAD_SIZE = 128
EXPERTS = 4
CAP = 32
EPS = 1e-05

CTX = ("zl", "core")
REQ = ("y", "x", "zh")


def route_tables(expert_ids, gate_num):
    blocks = expert_ids.shape[0]
    per_block = expert_ids.shape[1]
    top_k = expert_ids.shape[2]
    flat_ids = expert_ids.reshape(blocks, per_block * top_k)
    onehot = (flat_ids[..., None] == jnp.arange(EXPERTS, dtype=jnp.int32)).astype(jnp.int32)
    before = jnp.cumsum(onehot, axis=1) - onehot
    slot_num = jnp.sum(onehot * before, axis=-1)
    target = flat_ids * CAP + slot_num
    one_table = (target[..., None] == jnp.arange(EXPERTS * CAP, dtype=jnp.int32)).astype(
        jnp.float32
    )
    one_table = one_table.reshape(blocks, per_block, top_k, EXPERTS * CAP)
    fractions = gate_num.astype(jnp.float32) / 256.0
    dispatch = jnp.sum(one_table, axis=2)
    combine = jnp.sum(one_table * fractions[..., None], axis=2)
    return (dispatch, combine)


def attend_part(query_row_block, query_slot, key_row_block, value_row_block, key_slot):
    query_count = query_row_block.shape[0]
    key_count = key_row_block.shape[0]
    n_kv = key_row_block.shape[1] // HEAD_SIZE
    query_groups = query_row_block.shape[1] // HEAD_SIZE // n_kv
    query_head_rows = query_row_block.reshape(query_count, n_kv, query_groups, HEAD_SIZE)
    key_head_rows = key_row_block.reshape(key_count, n_kv, HEAD_SIZE)
    value_head_rows = value_row_block.reshape(key_count, n_kv, HEAD_SIZE)
    scores = jnp.einsum(
        "qhgd,khd->hgqk", query_head_rows, key_head_rows, preferred_element_type=jnp.float32
    ) * HEAD_SIZE ** (-0.5)
    capped = 30.0 * jnp.tanh(scores / 30.0)
    visible = key_slot[None, None, None, :] <= query_slot[None, None, :, None]
    attn_weights = jnp.where(visible, jnp.exp(capped), 0.0).astype(jnp.bfloat16)
    totals = jnp.sum(attn_weights.astype(jnp.float32), axis=-1)
    totals = jnp.transpose(totals, (2, 0, 1)).reshape(query_count, n_kv * query_groups)
    numerator = jnp.einsum(
        "hgqk,khd->qhgd", attn_weights, value_head_rows, preferred_element_type=jnp.float32
    )
    return (numerator.reshape(query_count, n_kv * query_groups * HEAD_SIZE), totals)


def col_slice(values, width):
    start = lax.axis_index(CTX) * width
    return lax.dynamic_slice_in_dim(values, start, width, values.ndim - 1)


def row_scale(local_rows, gain_cols):
    sum_sq = lax.psum(jnp.sum(local_rows * local_rows, axis=-1, keepdims=True), CTX)
    return local_rows * lax.rsqrt(sum_sq / D + EPS) * gain_cols


def per_device(
    queries,
    cached_keys,
    cached_values,
    fresh_keys,
    fresh_values,
    slot_order,
    residual,
    expert_ids,
    gate_num,
    gain_attn,
    gain_pre,
    gain_post,
    w_gate,
    w_up,
    w_down,
):
    query_row_block = queries[0]
    query_count = query_row_block.shape[0]
    width = query_row_block.shape[1]
    query_slot = slot_order[0].astype(jnp.float32)
    head_width = fresh_keys.shape[2]
    n_ctx = D // width

    with jax.named_scope("attention"):
        new_numer, new_totals = attend_part(
            query_row_block, query_slot, fresh_keys[0], fresh_values[0], query_slot
        )
        cache_rows = cached_keys.shape[1]
        both_heads = jnp.stack([cached_keys[0], cached_values[0]]).reshape(
            2, cache_rows, n_ctx, head_width
        )
        both_part = lax.all_to_all(both_heads, CTX, split_axis=2, concat_axis=1, tiled=True)
        key_part = both_part[0].reshape(-1, head_width)
        value_part = both_part[1].reshape(-1, head_width)
        cache_slot = jnp.full((key_part.shape[0],), -1.0, jnp.float32)
        numer_part, total_part = attend_part(
            query_row_block, query_slot, key_part, value_part, cache_slot
        )
        numerator = new_numer + numer_part
        totals = new_totals + total_part
        local_heads = (
            numerator.reshape(query_count, -1, HEAD_SIZE) / totals[..., None]
        ).reshape(query_count, -1)

    with jax.named_scope("norms"):
        residual_cols = col_slice(residual[0], width).astype(jnp.float32)
        hidden_cols = (residual_cols + row_scale(local_heads, col_slice(gain_attn, width))).astype(
            jnp.bfloat16
        )
        normed_cols = row_scale(hidden_cols.astype(jnp.float32), col_slice(gain_pre, width)).astype(
            jnp.bfloat16
        )

    dispatch, combine = route_tables(expert_ids, gate_num)
    n_zl = D // width // 2
    group = CAP // n_zl
    swap = [(0, 1), (1, 0)]
    with jax.named_scope("dispatch"):
        buffer = jnp.einsum(
            "ns,nd->sd",
            dispatch[0].astype(jnp.bfloat16),
            normed_cols,
            preferred_element_type=jnp.float32,
        ).astype(jnp.bfloat16)
        rows = buffer.reshape(EXPERTS * n_zl, group, width)
        rows = lax.all_to_all(rows, ("y", "zl"), split_axis=0, concat_axis=0, tiled=True)
        rows = jnp.transpose(rows.reshape(EXPERTS, n_zl, group, width), (0, 2, 1, 3))
        rows = lax.all_gather(rows, ("zh", "zl"), axis=0, tiled=True)
        block = rows.reshape(-1, n_zl * width)
        half = block.shape[0] // 2
        n_x = lax.axis_size("x")
        fwd = [(i, (i + 1) % n_x) for i in range(n_x)]
        bwd = [(i, (i - 1) % n_x) for i in range(n_x)]
        from_prev = lax.ppermute(block, "x", fwd)
        from_next = lax.ppermute(block, "x", bwd)
        far = jnp.concatenate(
            [lax.ppermute(from_prev[:half], "x", fwd), lax.ppermute(from_next[half:], "x", bwd)]
        )
        own_blocks = [block, from_next, far, from_prev]

    with jax.named_scope("experts"):
        core = lax.axis_index("core")

        def halves(mat, axis):
            shape = mat.shape
            split = shape[:axis] + (n_zl, 2, width) + shape[axis + 1 :]
            mat = mat.reshape(split)
            own = lax.dynamic_index_in_dim(mat, core, axis + 1, keepdims=False)
            other = lax.dynamic_index_in_dim(mat, 1 - core, axis + 1, keepdims=False)
            merged = shape[:axis] + (n_zl * width,) + shape[axis + 1 :]
            return own.reshape(merged), other.reshape(merged)

        gate_own, gate_other = halves(w_gate[0], 0)
        up_own, up_other = halves(w_up[0], 0)
        down_own, down_other = halves(w_down[0], 1)

        def expert_block(own_rows):
            other_rows = lax.ppermute(own_rows, "core", swap)
            pre_gate = jnp.dot(own_rows, gate_own, preferred_element_type=jnp.float32) + jnp.dot(
                other_rows, gate_other, preferred_element_type=jnp.float32
            )
            pre_up = jnp.dot(own_rows, up_own, preferred_element_type=jnp.float32) + jnp.dot(
                other_rows, up_other, preferred_element_type=jnp.float32
            )
            hidden_units = (jax.nn.gelu(pre_gate) * pre_up).astype(jnp.bfloat16)
            piece_own = jnp.dot(
                hidden_units, down_own, preferred_element_type=jnp.float32
            ).astype(jnp.bfloat16)
            piece_other = jnp.dot(
                hidden_units, down_other, preferred_element_type=jnp.float32
            ).astype(jnp.bfloat16)
            received = lax.ppermute(piece_other, "core", swap)
            return piece_own.astype(jnp.float32) + received.astype(jnp.float32)

        sums = [expert_block(b) for b in own_blocks]

    with jax.named_scope("combine"):
        to_next = lax.ppermute(sums[2][:half].astype(jnp.bfloat16), "x", fwd)
        to_prev = lax.ppermute(sums[2][half:].astype(jnp.bfloat16), "x", bwd)
        pad = jnp.zeros_like(to_next)
        send_next = (sums[1] + jnp.concatenate([to_next, pad]).astype(jnp.float32)).astype(
            jnp.bfloat16
        )
        send_prev = (sums[3] + jnp.concatenate([pad, to_prev]).astype(jnp.float32)).astype(
            jnp.bfloat16
        )
        got_prev = lax.ppermute(send_next, "x", fwd)
        got_next = lax.ppermute(send_prev, "x", bwd)
        parts = (
            sums[0] + got_prev.astype(jnp.float32) + got_next.astype(jnp.float32)
        ).astype(jnp.bfloat16)
        parts = parts.reshape(rows.shape)
        parts = parts.reshape((2 * n_zl, -1) + parts.shape[1:])
        parts = lax.psum_scatter(parts, ("zh", "zl"), scatter_dimension=0, tiled=False)
        parts = jnp.transpose(parts.reshape(EXPERTS, group, n_zl, width), (0, 2, 1, 3))
        parts = parts.reshape(EXPERTS * n_zl, group, width)
        outs = lax.all_to_all(parts, ("y", "zl"), split_axis=0, concat_axis=0, tiled=True)
        expert_cols = outs.reshape(EXPERTS * CAP, width).astype(jnp.float32)
        mixture = jnp.dot(combine[0], expert_cols, precision=lax.Precision.HIGHEST)
        layer_cols = (
            hidden_cols.astype(jnp.float32) + row_scale(mixture, col_slice(gain_post, width))
        ).astype(jnp.bfloat16)
        layer_out = lax.all_gather(layer_cols, CTX, axis=1, tiled=True)
    return layer_out[None]


def solution(mesh):
    n_exp = mesh.shape["exp"]
    n_ctx = mesh.shape["ctx"]
    sizes = {"y": EXPERTS, "x": n_exp // EXPERTS // 2, "zh": 2, "zl": n_ctx // 2, "core": 2}
    parts = {"exp": ("y", "x", "zh"), "ctx": ("zl", "core")}
    names = tuple(n for axis in mesh.axis_names for n in parts[axis])
    devices = np.asarray(mesh.devices).reshape(tuple(sizes[n] for n in names))
    fine = Mesh(devices, names)
    in_specs = (
        P(REQ, None, CTX),
        P(REQ, CTX, None),
        P(REQ, CTX, None),
        P(REQ, None, CTX),
        P(REQ, None, CTX),
        P(REQ, None),
        P(REQ, None, None),
        P(REQ, None, None),
        P(REQ, None, None),
        P(),
        P(),
        P(),
        P(REQ, None, CTX),
        P(REQ, None, CTX),
        P(REQ, CTX, None),
    )
    out_specs = P(REQ, None, None)
    return jax.shard_map(
        per_device, mesh=fine, in_specs=in_specs, out_specs=out_specs, check_vma=False
    )
```

```python
import jax
import jax.numpy as jnp
import numpy as np
from jax import lax
from jax.sharding import Mesh
from jax.sharding import PartitionSpec as P

D = 6144
HEAD_SIZE = 128
EXPERTS = 4
CAP = 32
EPS = 1e-05

CTX = ("zl", "core")
REQ = ("y", "x", "zh")
Z_AXES = ("zl", "zh")


def route_tables(expert_ids, gate_num):
    blocks = expert_ids.shape[0]
    per_block = expert_ids.shape[1]
    top_k = expert_ids.shape[2]
    flat_ids = expert_ids.reshape(blocks, per_block * top_k)
    onehot = (flat_ids[..., None] == jnp.arange(EXPERTS, dtype=jnp.int32)).astype(jnp.int32)
    before = jnp.cumsum(onehot, axis=1) - onehot
    slot_num = jnp.sum(onehot * before, axis=-1)
    target = flat_ids * CAP + slot_num
    one_table = (target[..., None] == jnp.arange(EXPERTS * CAP, dtype=jnp.int32)).astype(
        jnp.float32
    )
    one_table = one_table.reshape(blocks, per_block, top_k, EXPERTS * CAP)
    fractions = gate_num.astype(jnp.float32) / 256.0
    dispatch = jnp.sum(one_table, axis=2)
    combine = jnp.sum(one_table * fractions[..., None], axis=2)
    return (dispatch, combine)


def attend_part(query_row_block, query_slot, key_row_block, value_row_block, key_slot):
    query_count = query_row_block.shape[0]
    key_count = key_row_block.shape[0]
    n_kv = key_row_block.shape[1] // HEAD_SIZE
    query_groups = query_row_block.shape[1] // HEAD_SIZE // n_kv
    query_head_rows = query_row_block.reshape(query_count, n_kv, query_groups, HEAD_SIZE)
    key_head_rows = key_row_block.reshape(key_count, n_kv, HEAD_SIZE)
    value_head_rows = value_row_block.reshape(key_count, n_kv, HEAD_SIZE)
    scores = jnp.einsum(
        "qhgd,khd->hgqk", query_head_rows, key_head_rows, preferred_element_type=jnp.float32
    ) * HEAD_SIZE ** (-0.5)
    capped = 30.0 * jnp.tanh(scores / 30.0)
    visible = key_slot[None, None, None, :] <= query_slot[None, None, :, None]
    attn_weights = jnp.where(visible, jnp.exp(capped), 0.0).astype(jnp.bfloat16)
    totals = jnp.sum(attn_weights.astype(jnp.float32), axis=-1)
    totals = jnp.transpose(totals, (2, 0, 1)).reshape(query_count, n_kv * query_groups)
    numerator = jnp.einsum(
        "hgqk,khd->qhgd", attn_weights, value_head_rows, preferred_element_type=jnp.float32
    )
    return (numerator.reshape(query_count, n_kv * query_groups * HEAD_SIZE), totals)


def col_slice(values, width):
    start = lax.axis_index(CTX) * width
    return lax.dynamic_slice_in_dim(values, start, width, values.ndim - 1)


def row_scale(local_rows, gain_cols):
    sum_sq = lax.psum(jnp.sum(local_rows * local_rows, axis=-1, keepdims=True), CTX)
    return local_rows * lax.rsqrt(sum_sq / D + EPS) * gain_cols


def ring_perms(n, place):
    fwd = [(place[i], place[(i + 1) % n]) for i in range(n)]
    bwd = [(place[i], place[(i - 1) % n]) for i in range(n)]
    return fwd, bwd


def ring_gather(block, axis, n, place):
    fwd, bwd = ring_perms(n, place)
    half = block.shape[0] // 2
    out = [None] * n
    out[0] = block
    from_prev = block
    from_next = block
    for d in range(1, n // 2 + 1):
        if 2 * d == n:
            out[d] = jnp.concatenate(
                [
                    lax.ppermute(from_prev[:half], axis, fwd),
                    lax.ppermute(from_next[half:], axis, bwd),
                ]
            )
        else:
            from_prev = lax.ppermute(from_prev, axis, fwd)
            from_next = lax.ppermute(from_next, axis, bwd)
            out[n - d] = from_prev
            out[d] = from_next
    return out


def ring_reduce(parts, axis, n, place):
    fwd, bwd = ring_perms(n, place)
    far = n // 2
    half = parts[0].shape[0] // 2
    got_prev = lax.ppermute(parts[far][:half].astype(jnp.bfloat16), axis, fwd)
    got_next = lax.ppermute(parts[far][half:].astype(jnp.bfloat16), axis, bwd)
    pad = jnp.zeros_like(got_prev)
    got_prev = jnp.concatenate([got_prev, pad])
    got_next = jnp.concatenate([pad, got_next])
    for d in range(far - 1, 0, -1):
        send_next = (parts[d] + got_prev.astype(jnp.float32)).astype(jnp.bfloat16)
        send_prev = (parts[n - d] + got_next.astype(jnp.float32)).astype(jnp.bfloat16)
        got_prev = lax.ppermute(send_next, axis, fwd)
        got_next = lax.ppermute(send_prev, axis, bwd)
    return parts[0] + got_prev.astype(jnp.float32) + got_next.astype(jnp.float32)


def per_device(
    queries,
    cached_keys,
    cached_values,
    fresh_keys,
    fresh_values,
    slot_order,
    residual,
    expert_ids,
    gate_num,
    gain_attn,
    gain_pre,
    gain_post,
    w_gate,
    w_up,
    w_down,
):
    query_row_block = queries[0]
    query_count = query_row_block.shape[0]
    width = query_row_block.shape[1]
    query_slot = slot_order[0].astype(jnp.float32)
    head_width = fresh_keys.shape[2]
    n_ctx = D // width

    with jax.named_scope("attention"):
        new_numer, new_totals = attend_part(
            query_row_block, query_slot, fresh_keys[0], fresh_values[0], query_slot
        )
        cache_rows = cached_keys.shape[1]
        both_heads = jnp.stack([cached_keys[0], cached_values[0]]).reshape(
            2, cache_rows, n_ctx, head_width
        )
        both_part = lax.all_to_all(both_heads, CTX, split_axis=2, concat_axis=1, tiled=True)
        key_part = both_part[0].reshape(-1, head_width)
        value_part = both_part[1].reshape(-1, head_width)
        cache_slot = jnp.full((key_part.shape[0],), -1.0, jnp.float32)
        numer_part, total_part = attend_part(
            query_row_block, query_slot, key_part, value_part, cache_slot
        )
        numerator = new_numer + numer_part
        totals = new_totals + total_part
        local_heads = (
            numerator.reshape(query_count, -1, HEAD_SIZE) / totals[..., None]
        ).reshape(query_count, -1)

    with jax.named_scope("norms"):
        residual_cols = col_slice(residual[0], width).astype(jnp.float32)
        hidden_cols = (residual_cols + row_scale(local_heads, col_slice(gain_attn, width))).astype(
            jnp.bfloat16
        )
        normed_cols = row_scale(hidden_cols.astype(jnp.float32), col_slice(gain_pre, width)).astype(
            jnp.bfloat16
        )

    dispatch, combine = route_tables(expert_ids, gate_num)
    n_zl = D // width // 2
    group = CAP // n_zl
    swap = [(0, 1), (1, 0)]
    with jax.named_scope("dispatch"):
        buffer = jnp.einsum(
            "ns,nd->sd",
            dispatch[0].astype(jnp.bfloat16),
            normed_cols,
            preferred_element_type=jnp.float32,
        ).astype(jnp.bfloat16)
        rows = buffer.reshape(EXPERTS * n_zl, group, width)
        rows = lax.all_to_all(rows, ("y", "zl"), split_axis=0, concat_axis=0, tiled=True)
        rows = jnp.transpose(rows.reshape(EXPERTS, n_zl, group, width), (0, 2, 1, 3))
        n_x = lax.axis_size("x")
        n_z = 2 * n_zl
        z_place = [(z % n_zl) * 2 + z // n_zl for z in range(n_z)]
        x_place = list(range(n_x))
        z_blocks = ring_gather(rows.reshape(-1, n_zl * width), Z_AXES, n_z, z_place)
        block = jnp.concatenate(z_blocks)
        own_blocks = ring_gather(block, "x", n_x, x_place)

    with jax.named_scope("experts"):
        core = lax.axis_index("core")

        def halves(mat, axis):
            shape = mat.shape
            split = shape[:axis] + (n_zl, 2, width) + shape[axis + 1 :]
            mat = mat.reshape(split)
            own = lax.dynamic_index_in_dim(mat, core, axis + 1, keepdims=False)
            other = lax.dynamic_index_in_dim(mat, 1 - core, axis + 1, keepdims=False)
            merged = shape[:axis] + (n_zl * width,) + shape[axis + 1 :]
            return own.reshape(merged), other.reshape(merged)

        gate_own, gate_other = halves(w_gate[0], 0)
        up_own, up_other = halves(w_up[0], 0)
        down_own, down_other = halves(w_down[0], 1)

        def expert_block(own_rows):
            other_rows = lax.ppermute(own_rows, "core", swap)
            pre_gate = jnp.dot(own_rows, gate_own, preferred_element_type=jnp.float32) + jnp.dot(
                other_rows, gate_other, preferred_element_type=jnp.float32
            )
            pre_up = jnp.dot(own_rows, up_own, preferred_element_type=jnp.float32) + jnp.dot(
                other_rows, up_other, preferred_element_type=jnp.float32
            )
            hidden_units = (jax.nn.gelu(pre_gate) * pre_up).astype(jnp.bfloat16)
            piece_own = jnp.dot(
                hidden_units, down_own, preferred_element_type=jnp.float32
            ).astype(jnp.bfloat16)
            piece_other = jnp.dot(
                hidden_units, down_other, preferred_element_type=jnp.float32
            ).astype(jnp.bfloat16)
            received = lax.ppermute(piece_other, "core", swap)
            return piece_own.astype(jnp.float32) + received.astype(jnp.float32)

        sums = [expert_block(b) for b in own_blocks]

    with jax.named_scope("combine"):
        x_sum = ring_reduce(sums, "x", n_x, x_place)
        z_parts = jnp.split(x_sum, n_z)
        parts = ring_reduce(z_parts, Z_AXES, n_z, z_place).astype(jnp.bfloat16)
        parts = jnp.transpose(parts.reshape(EXPERTS, group, n_zl, width), (0, 2, 1, 3))
        parts = parts.reshape(EXPERTS * n_zl, group, width)
        outs = lax.all_to_all(parts, ("y", "zl"), split_axis=0, concat_axis=0, tiled=True)
        expert_cols = outs.reshape(EXPERTS * CAP, width).astype(jnp.float32)
        mixture = jnp.dot(combine[0], expert_cols, precision=lax.Precision.HIGHEST)
        layer_cols = (
            hidden_cols.astype(jnp.float32) + row_scale(mixture, col_slice(gain_post, width))
        ).astype(jnp.bfloat16)
        layer_out = lax.all_gather(layer_cols, CTX, axis=1, tiled=True)
    return layer_out[None]


def solution(mesh):
    n_exp = mesh.shape["exp"]
    n_ctx = mesh.shape["ctx"]
    sizes = {"y": EXPERTS, "x": n_exp // EXPERTS // 2, "zh": 2, "zl": n_ctx // 2, "core": 2}
    parts = {"exp": ("y", "x", "zh"), "ctx": ("zl", "core")}
    names = tuple(n for axis in mesh.axis_names for n in parts[axis])
    devices = np.asarray(mesh.devices).reshape(tuple(sizes[n] for n in names))
    fine = Mesh(devices, names)
    in_specs = (
        P(REQ, None, CTX),
        P(REQ, CTX, None),
        P(REQ, CTX, None),
        P(REQ, None, CTX),
        P(REQ, None, CTX),
        P(REQ, None),
        P(REQ, None, None),
        P(REQ, None, None),
        P(REQ, None, None),
        P(),
        P(),
        P(),
        P(REQ, None, CTX),
        P(REQ, None, CTX),
        P(REQ, CTX, None),
    )
    out_specs = P(REQ, None, None)
    return jax.shard_map(
        per_device, mesh=fine, in_specs=in_specs, out_specs=out_specs, check_vma=False
    )
```

```python
import jax
import jax.numpy as jnp
import numpy as np
from jax import lax
from jax.sharding import Mesh
from jax.sharding import PartitionSpec as P

D = 6144
HEAD_SIZE = 128
EXPERTS = 4
CAP = 32
EPS = 1e-05

CTX = ("zl", "core")
REQ = ("y", "x", "zh")
Z_AXES = ("zl", "zh")


def route_tables(expert_ids, gate_num):
    blocks = expert_ids.shape[0]
    per_block = expert_ids.shape[1]
    top_k = expert_ids.shape[2]
    flat_ids = expert_ids.reshape(blocks, per_block * top_k)
    onehot = (flat_ids[..., None] == jnp.arange(EXPERTS, dtype=jnp.int32)).astype(jnp.int32)
    before = jnp.cumsum(onehot, axis=1) - onehot
    slot_num = jnp.sum(onehot * before, axis=-1)
    target = flat_ids * CAP + slot_num
    one_table = (target[..., None] == jnp.arange(EXPERTS * CAP, dtype=jnp.int32)).astype(
        jnp.float32
    )
    one_table = one_table.reshape(blocks, per_block, top_k, EXPERTS * CAP)
    fractions = gate_num.astype(jnp.float32) / 256.0
    dispatch = jnp.sum(one_table, axis=2)
    combine = jnp.sum(one_table * fractions[..., None], axis=2)
    return (dispatch, combine)


def attend_part(query_row_block, query_slot, key_row_block, value_row_block, key_slot):
    query_count = query_row_block.shape[0]
    key_count = key_row_block.shape[0]
    n_kv = key_row_block.shape[1] // HEAD_SIZE
    query_groups = query_row_block.shape[1] // HEAD_SIZE // n_kv
    query_head_rows = query_row_block.reshape(query_count, n_kv, query_groups, HEAD_SIZE)
    key_head_rows = key_row_block.reshape(key_count, n_kv, HEAD_SIZE)
    value_head_rows = value_row_block.reshape(key_count, n_kv, HEAD_SIZE)
    scores = jnp.einsum(
        "qhgd,khd->hgqk", query_head_rows, key_head_rows, preferred_element_type=jnp.float32
    ) * HEAD_SIZE ** (-0.5)
    capped = 30.0 * jnp.tanh(scores / 30.0)
    visible = key_slot[None, None, None, :] <= query_slot[None, None, :, None]
    attn_weights = jnp.where(visible, jnp.exp(capped), 0.0).astype(jnp.bfloat16)
    totals = jnp.sum(attn_weights.astype(jnp.float32), axis=-1)
    totals = jnp.transpose(totals, (2, 0, 1)).reshape(query_count, n_kv * query_groups)
    numerator = jnp.einsum(
        "hgqk,khd->qhgd", attn_weights, value_head_rows, preferred_element_type=jnp.float32
    )
    return (numerator.reshape(query_count, n_kv * query_groups * HEAD_SIZE), totals)


def col_slice(values, width):
    start = lax.axis_index(CTX) * width
    return lax.dynamic_slice_in_dim(values, start, width, values.ndim - 1)


def row_scale(local_rows, gain_cols):
    sum_sq = lax.psum(jnp.sum(local_rows * local_rows, axis=-1, keepdims=True), CTX)
    return local_rows * lax.rsqrt(sum_sq / D + EPS) * gain_cols


def ring_perms(n, place):
    fwd = [(place[i], place[(i + 1) % n]) for i in range(n)]
    bwd = [(place[i], place[(i - 1) % n]) for i in range(n)]
    return fwd, bwd


def ring_gather(block, axis, n, place):
    fwd, bwd = ring_perms(n, place)
    half = block.shape[0] // 2
    out = [None] * n
    out[0] = block
    from_prev = block
    from_next = block
    for d in range(1, n // 2 + 1):
        if 2 * d == n:
            out[d] = jnp.concatenate(
                [
                    lax.ppermute(from_prev[:half], axis, fwd),
                    lax.ppermute(from_next[half:], axis, bwd),
                ]
            )
        else:
            from_prev = lax.ppermute(from_prev, axis, fwd)
            from_next = lax.ppermute(from_next, axis, bwd)
            out[n - d] = from_prev
            out[d] = from_next
    return out


def ring_reduce(parts, axis, n, place):
    fwd, bwd = ring_perms(n, place)
    far = n // 2
    half = parts[0].shape[0] // 2
    got_prev = lax.ppermute(parts[far][:half].astype(jnp.bfloat16), axis, fwd)
    got_next = lax.ppermute(parts[far][half:].astype(jnp.bfloat16), axis, bwd)
    pad = jnp.zeros_like(got_prev)
    got_prev = jnp.concatenate([got_prev, pad])
    got_next = jnp.concatenate([pad, got_next])
    for d in range(far - 1, 0, -1):
        send_next = (parts[d] + got_prev.astype(jnp.float32)).astype(jnp.bfloat16)
        send_prev = (parts[n - d] + got_next.astype(jnp.float32)).astype(jnp.bfloat16)
        got_prev = lax.ppermute(send_next, axis, fwd)
        got_next = lax.ppermute(send_prev, axis, bwd)
    return parts[0] + got_prev.astype(jnp.float32) + got_next.astype(jnp.float32)


def per_device(
    queries,
    cached_keys,
    cached_values,
    fresh_keys,
    fresh_values,
    slot_order,
    residual,
    expert_ids,
    gate_num,
    gain_attn,
    gain_pre,
    gain_post,
    w_gate,
    w_up,
    w_down,
):
    query_row_block = queries[0]
    query_count = query_row_block.shape[0]
    width = query_row_block.shape[1]
    query_slot = slot_order[0].astype(jnp.float32)
    head_width = fresh_keys.shape[2]
    n_ctx = D // width

    with jax.named_scope("attention"):
        new_numer, new_totals = attend_part(
            query_row_block, query_slot, fresh_keys[0], fresh_values[0], query_slot
        )
        cache_rows = cached_keys.shape[1]
        both_heads = jnp.stack([cached_keys[0], cached_values[0]]).reshape(
            2, cache_rows, n_ctx, head_width
        )
        both_part = lax.all_to_all(both_heads, CTX, split_axis=2, concat_axis=1, tiled=True)
        key_part = both_part[0].reshape(-1, head_width)
        value_part = both_part[1].reshape(-1, head_width)
        cache_slot = jnp.full((key_part.shape[0],), -1.0, jnp.float32)
        numer_part, total_part = attend_part(
            query_row_block, query_slot, key_part, value_part, cache_slot
        )
        numerator = new_numer + numer_part
        totals = new_totals + total_part
        local_heads = (
            numerator.reshape(query_count, -1, HEAD_SIZE) / totals[..., None]
        ).reshape(query_count, -1)

    with jax.named_scope("norms"):
        residual_cols = col_slice(residual[0], width).astype(jnp.float32)
        hidden_cols = (residual_cols + row_scale(local_heads, col_slice(gain_attn, width))).astype(
            jnp.bfloat16
        )
        normed_cols = row_scale(hidden_cols.astype(jnp.float32), col_slice(gain_pre, width)).astype(
            jnp.bfloat16
        )

    dispatch, combine = route_tables(expert_ids, gate_num)
    n_zl = D // width // 2
    group = CAP // n_zl
    swap = [(0, 1), (1, 0)]
    with jax.named_scope("dispatch"):
        buffer = jnp.einsum(
            "ns,nd->sd",
            dispatch[0].astype(jnp.bfloat16),
            normed_cols,
            preferred_element_type=jnp.float32,
        ).astype(jnp.bfloat16)
        rows = buffer.reshape(EXPERTS * n_zl, group, width)
        rows = lax.all_to_all(rows, ("y", "zl"), split_axis=0, concat_axis=0, tiled=True)
        rows = jnp.transpose(rows.reshape(EXPERTS, n_zl, group, width), (0, 2, 1, 3))
        n_x = lax.axis_size("x")
        n_z = 2 * n_zl
        z_place = [(z % n_zl) * 2 + z // n_zl for z in range(n_z)]
        x_place = list(range(n_x))
        cut = group // 2
        first = rows[:, :cut].reshape(-1, n_zl * width)
        second = rows[:, cut:].reshape(-1, n_zl * width)
        first = jnp.concatenate(ring_gather(first, Z_AXES, n_z, z_place))
        first = jnp.concatenate(ring_gather(first, "x", n_x, x_place))
        second = jnp.concatenate(ring_gather(second, "x", n_x, x_place))
        second = jnp.concatenate(ring_gather(second, Z_AXES, n_z, z_place))

    with jax.named_scope("experts"):
        core = lax.axis_index("core")

        def halves(mat, axis):
            shape = mat.shape
            split = shape[:axis] + (n_zl, 2, width) + shape[axis + 1 :]
            mat = mat.reshape(split)
            own = lax.dynamic_index_in_dim(mat, core, axis + 1, keepdims=False)
            other = lax.dynamic_index_in_dim(mat, 1 - core, axis + 1, keepdims=False)
            merged = shape[:axis] + (n_zl * width,) + shape[axis + 1 :]
            return own.reshape(merged), other.reshape(merged)

        gate_own, gate_other = halves(w_gate[0], 0)
        up_own, up_other = halves(w_up[0], 0)
        down_own, down_other = halves(w_down[0], 1)

        def expert_block(own_rows):
            other_rows = lax.ppermute(own_rows, "core", swap)
            pre_gate = jnp.dot(own_rows, gate_own, preferred_element_type=jnp.float32) + jnp.dot(
                other_rows, gate_other, preferred_element_type=jnp.float32
            )
            pre_up = jnp.dot(own_rows, up_own, preferred_element_type=jnp.float32) + jnp.dot(
                other_rows, up_other, preferred_element_type=jnp.float32
            )
            hidden_units = (jax.nn.gelu(pre_gate) * pre_up).astype(jnp.bfloat16)
            piece_own = jnp.dot(
                hidden_units, down_own, preferred_element_type=jnp.float32
            ).astype(jnp.bfloat16)
            piece_other = jnp.dot(
                hidden_units, down_other, preferred_element_type=jnp.float32
            ).astype(jnp.bfloat16)
            received = lax.ppermute(piece_other, "core", swap)
            return piece_own.astype(jnp.float32) + received.astype(jnp.float32)

        first_sum = expert_block(first)
        second_sum = expert_block(second)

    with jax.named_scope("combine"):
        first_sum = ring_reduce(jnp.split(first_sum, n_x), "x", n_x, x_place)
        first_sum = ring_reduce(jnp.split(first_sum, n_z), Z_AXES, n_z, z_place)
        second_sum = ring_reduce(jnp.split(second_sum, n_z), Z_AXES, n_z, z_place)
        second_sum = ring_reduce(jnp.split(second_sum, n_x), "x", n_x, x_place)
        parts = jnp.concatenate(
            [
                first_sum.reshape(EXPERTS, cut, n_zl, width),
                second_sum.reshape(EXPERTS, group - cut, n_zl, width),
            ],
            axis=1,
        ).astype(jnp.bfloat16)
        parts = jnp.transpose(parts.reshape(EXPERTS, group, n_zl, width), (0, 2, 1, 3))
        parts = parts.reshape(EXPERTS * n_zl, group, width)
        outs = lax.all_to_all(parts, ("y", "zl"), split_axis=0, concat_axis=0, tiled=True)
        expert_cols = outs.reshape(EXPERTS * CAP, width).astype(jnp.float32)
        mixture = jnp.dot(combine[0], expert_cols, precision=lax.Precision.HIGHEST)
        layer_cols = (
            hidden_cols.astype(jnp.float32) + row_scale(mixture, col_slice(gain_post, width))
        ).astype(jnp.bfloat16)
        layer_out = lax.all_gather(layer_cols, CTX, axis=1, tiled=True)
    return layer_out[None]


def solution(mesh):
    n_exp = mesh.shape["exp"]
    n_ctx = mesh.shape["ctx"]
    sizes = {"y": EXPERTS, "x": n_exp // EXPERTS // 2, "zh": 2, "zl": n_ctx // 2, "core": 2}
    parts = {"exp": ("y", "x", "zh"), "ctx": ("zl", "core")}
    names = tuple(n for axis in mesh.axis_names for n in parts[axis])
    devices = np.asarray(mesh.devices).reshape(tuple(sizes[n] for n in names))
    fine = Mesh(devices, names)
    in_specs = (
        P(REQ, None, CTX),
        P(REQ, CTX, None),
        P(REQ, CTX, None),
        P(REQ, None, CTX),
        P(REQ, None, CTX),
        P(REQ, None),
        P(REQ, None, None),
        P(REQ, None, None),
        P(REQ, None, None),
        P(),
        P(),
        P(),
        P(REQ, None, CTX),
        P(REQ, None, CTX),
        P(REQ, CTX, None),
    )
    out_specs = P(REQ, None, None)
    return jax.shard_map(
        per_device, mesh=fine, in_specs=in_specs, out_specs=out_specs, check_vma=False
    )
```

```python
import jax
import jax.numpy as jnp
import numpy as np
from jax import lax
from jax.sharding import Mesh
from jax.sharding import PartitionSpec as P

D = 6144
HEAD_SIZE = 128
EXPERTS = 4
CAP = 32
EPS = 1e-05

CTX = ("zl", "core")
REQ = ("y", "x", "zh")
Z_AXES = ("zl", "zh")


def route_tables(expert_ids, gate_num):
    blocks = expert_ids.shape[0]
    per_block = expert_ids.shape[1]
    top_k = expert_ids.shape[2]
    flat_ids = expert_ids.reshape(blocks, per_block * top_k)
    onehot = (flat_ids[..., None] == jnp.arange(EXPERTS, dtype=jnp.int32)).astype(jnp.int32)
    before = jnp.cumsum(onehot, axis=1) - onehot
    slot_num = jnp.sum(onehot * before, axis=-1)
    target = flat_ids * CAP + slot_num
    one_table = (target[..., None] == jnp.arange(EXPERTS * CAP, dtype=jnp.int32)).astype(
        jnp.float32
    )
    one_table = one_table.reshape(blocks, per_block, top_k, EXPERTS * CAP)
    fractions = gate_num.astype(jnp.float32) / 256.0
    dispatch = jnp.sum(one_table, axis=2)
    combine = jnp.sum(one_table * fractions[..., None], axis=2)
    return (dispatch, combine)


def attend_part(query_row_block, query_slot, key_row_block, value_row_block, key_slot):
    query_count = query_row_block.shape[0]
    key_count = key_row_block.shape[0]
    n_kv = key_row_block.shape[1] // HEAD_SIZE
    query_groups = query_row_block.shape[1] // HEAD_SIZE // n_kv
    query_head_rows = query_row_block.reshape(query_count, n_kv, query_groups, HEAD_SIZE)
    key_head_rows = key_row_block.reshape(key_count, n_kv, HEAD_SIZE)
    value_head_rows = value_row_block.reshape(key_count, n_kv, HEAD_SIZE)
    scores = jnp.einsum(
        "qhgd,khd->hgqk", query_head_rows, key_head_rows, preferred_element_type=jnp.float32
    ) * HEAD_SIZE ** (-0.5)
    capped = 30.0 * jnp.tanh(scores / 30.0)
    visible = key_slot[None, None, None, :] <= query_slot[None, None, :, None]
    attn_weights = jnp.where(visible, jnp.exp(capped), 0.0).astype(jnp.bfloat16)
    totals = jnp.sum(attn_weights.astype(jnp.float32), axis=-1)
    totals = jnp.transpose(totals, (2, 0, 1)).reshape(query_count, n_kv * query_groups)
    numerator = jnp.einsum(
        "hgqk,khd->qhgd", attn_weights, value_head_rows, preferred_element_type=jnp.float32
    )
    return (numerator.reshape(query_count, n_kv * query_groups * HEAD_SIZE), totals)


def col_slice(values, width):
    start = lax.axis_index(CTX) * width
    return lax.dynamic_slice_in_dim(values, start, width, values.ndim - 1)


def row_scale(local_rows, gain_cols):
    sum_sq = lax.psum(jnp.sum(local_rows * local_rows, axis=-1, keepdims=True), CTX)
    return local_rows * lax.rsqrt(sum_sq / D + EPS) * gain_cols


def ring_perms(n, place):
    fwd = [(place[i], place[(i + 1) % n]) for i in range(n)]
    bwd = [(place[i], place[(i - 1) % n]) for i in range(n)]
    return fwd, bwd


def ring_gather(block, axis, n, place):
    fwd, bwd = ring_perms(n, place)
    half = block.shape[0] // 2
    out = [None] * n
    out[0] = block
    from_prev = block
    from_next = block
    for d in range(1, n // 2 + 1):
        if 2 * d == n:
            out[d] = jnp.concatenate(
                [
                    lax.ppermute(from_prev[:half], axis, fwd),
                    lax.ppermute(from_next[half:], axis, bwd),
                ]
            )
        else:
            from_prev = lax.ppermute(from_prev, axis, fwd)
            from_next = lax.ppermute(from_next, axis, bwd)
            out[n - d] = from_prev
            out[d] = from_next
    return out


def ring_reduce(parts, axis, n, place):
    fwd, bwd = ring_perms(n, place)
    far = n // 2
    half = parts[0].shape[0] // 2
    got_prev = lax.ppermute(parts[far][:half].astype(jnp.bfloat16), axis, fwd)
    got_next = lax.ppermute(parts[far][half:].astype(jnp.bfloat16), axis, bwd)
    pad = jnp.zeros_like(got_prev)
    got_prev = jnp.concatenate([got_prev, pad])
    got_next = jnp.concatenate([pad, got_next])
    for d in range(far - 1, 0, -1):
        send_next = (parts[d] + got_prev.astype(jnp.float32)).astype(jnp.bfloat16)
        send_prev = (parts[n - d] + got_next.astype(jnp.float32)).astype(jnp.bfloat16)
        got_prev = lax.ppermute(send_next, axis, fwd)
        got_next = lax.ppermute(send_prev, axis, bwd)
    return parts[0] + got_prev.astype(jnp.float32) + got_next.astype(jnp.float32)


def per_device(
    queries,
    cached_keys,
    cached_values,
    fresh_keys,
    fresh_values,
    slot_order,
    residual,
    expert_ids,
    gate_num,
    gain_attn,
    gain_pre,
    gain_post,
    w_gate,
    w_up,
    w_down,
):
    query_row_block = queries[0]
    query_count = query_row_block.shape[0]
    width = query_row_block.shape[1]
    query_slot = slot_order[0].astype(jnp.float32)
    head_width = fresh_keys.shape[2]
    n_ctx = D // width

    with jax.named_scope("attention"):
        new_numer, new_totals = attend_part(
            query_row_block, query_slot, fresh_keys[0], fresh_values[0], query_slot
        )
        cache_rows = cached_keys.shape[1]
        both_heads = jnp.stack([cached_keys[0], cached_values[0]]).reshape(
            2, cache_rows, n_ctx, head_width
        )
        both_part = lax.all_to_all(both_heads, CTX, split_axis=2, concat_axis=1, tiled=True)
        key_part = both_part[0].reshape(-1, head_width)
        value_part = both_part[1].reshape(-1, head_width)
        cache_slot = jnp.full((key_part.shape[0],), -1.0, jnp.float32)
        numer_part, total_part = attend_part(
            query_row_block, query_slot, key_part, value_part, cache_slot
        )
        numerator = new_numer + numer_part
        totals = new_totals + total_part
        local_heads = (
            numerator.reshape(query_count, -1, HEAD_SIZE) / totals[..., None]
        ).reshape(query_count, -1)

    with jax.named_scope("norms"):
        residual_cols = col_slice(residual[0], width).astype(jnp.float32)
        hidden_cols = (residual_cols + row_scale(local_heads, col_slice(gain_attn, width))).astype(
            jnp.bfloat16
        )
        normed_cols = row_scale(hidden_cols.astype(jnp.float32), col_slice(gain_pre, width)).astype(
            jnp.bfloat16
        )

    dispatch, combine = route_tables(expert_ids, gate_num)
    n_zl = D // width // 2
    group = CAP // n_zl
    swap = [(0, 1), (1, 0)]
    with jax.named_scope("dispatch"):
        buffer = jnp.einsum(
            "ns,nd->sd",
            dispatch[0].astype(jnp.bfloat16),
            normed_cols,
            preferred_element_type=jnp.float32,
        ).astype(jnp.bfloat16)
        rows = buffer.reshape(EXPERTS * n_zl, group, width)
        rows = lax.all_to_all(rows, ("y", "zl"), split_axis=0, concat_axis=0, tiled=True)
        rows = jnp.transpose(rows.reshape(EXPERTS, n_zl, group, width), (0, 2, 1, 3))
        n_x = lax.axis_size("x")
        n_z = 2 * n_zl
        z_place = [(z % n_zl) * 2 + z // n_zl for z in range(n_z)]
        x_place = list(range(n_x))
        z_blocks = ring_gather(rows.reshape(-1, n_zl * width), Z_AXES, n_z, z_place)
        block = jnp.concatenate(z_blocks)
        own_blocks = ring_gather(block, "x", n_x, x_place)

    with jax.named_scope("experts"):
        core = lax.axis_index("core")

        def halves(mat, axis):
            shape = mat.shape
            split = shape[:axis] + (n_zl, 2, width) + shape[axis + 1 :]
            mat = mat.reshape(split)
            own = lax.dynamic_index_in_dim(mat, core, axis + 1, keepdims=False)
            other = lax.dynamic_index_in_dim(mat, 1 - core, axis + 1, keepdims=False)
            merged = shape[:axis] + (n_zl * width,) + shape[axis + 1 :]
            return own.reshape(merged), other.reshape(merged)

        gate_own, gate_other = halves(w_gate[0], 0)
        up_own, up_other = halves(w_up[0], 0)
        down_own, down_other = halves(w_down[0], 1)

        def expert_block(own_rows):
            other_rows = lax.ppermute(own_rows, "core", swap)
            pre_gate = jnp.dot(own_rows, gate_own, preferred_element_type=jnp.float32) + jnp.dot(
                other_rows, gate_other, preferred_element_type=jnp.float32
            )
            pre_up = jnp.dot(own_rows, up_own, preferred_element_type=jnp.float32) + jnp.dot(
                other_rows, up_other, preferred_element_type=jnp.float32
            )
            hidden_units = (jax.nn.gelu(pre_gate) * pre_up).astype(jnp.bfloat16)
            piece_own = jnp.dot(
                hidden_units, down_own, preferred_element_type=jnp.float32
            ).astype(jnp.bfloat16)
            piece_other = jnp.dot(
                hidden_units, down_other, preferred_element_type=jnp.float32
            ).astype(jnp.bfloat16)
            received = lax.ppermute(piece_other, "core", swap)
            return piece_own.astype(jnp.float32) + received.astype(jnp.float32)

        sums = jnp.split(expert_block(jnp.concatenate(own_blocks)), n_x)

    with jax.named_scope("combine"):
        x_sum = ring_reduce(sums, "x", n_x, x_place)
        z_parts = jnp.split(x_sum, n_z)
        parts = ring_reduce(z_parts, Z_AXES, n_z, z_place).astype(jnp.bfloat16)
        parts = jnp.transpose(parts.reshape(EXPERTS, group, n_zl, width), (0, 2, 1, 3))
        parts = parts.reshape(EXPERTS * n_zl, group, width)
        outs = lax.all_to_all(parts, ("y", "zl"), split_axis=0, concat_axis=0, tiled=True)
        expert_cols = outs.reshape(EXPERTS * CAP, width).astype(jnp.float32)
        mixture = jnp.dot(combine[0], expert_cols, precision=lax.Precision.HIGHEST)
        layer_cols = (
            hidden_cols.astype(jnp.float32) + row_scale(mixture, col_slice(gain_post, width))
        ).astype(jnp.bfloat16)
        layer_out = lax.all_gather(layer_cols, CTX, axis=1, tiled=True)
    return layer_out[None]


def solution(mesh):
    n_exp = mesh.shape["exp"]
    n_ctx = mesh.shape["ctx"]
    sizes = {"y": EXPERTS, "x": n_exp // EXPERTS // 2, "zh": 2, "zl": n_ctx // 2, "core": 2}
    parts = {"exp": ("y", "x", "zh"), "ctx": ("zl", "core")}
    names = tuple(n for axis in mesh.axis_names for n in parts[axis])
    devices = np.asarray(mesh.devices).reshape(tuple(sizes[n] for n in names))
    fine = Mesh(devices, names)
    in_specs = (
        P(REQ, None, CTX),
        P(REQ, CTX, None),
        P(REQ, CTX, None),
        P(REQ, None, CTX),
        P(REQ, None, CTX),
        P(REQ, None),
        P(REQ, None, None),
        P(REQ, None, None),
        P(REQ, None, None),
        P(),
        P(),
        P(),
        P(REQ, None, CTX),
        P(REQ, None, CTX),
        P(REQ, CTX, None),
    )
    out_specs = P(REQ, None, None)
    return jax.shard_map(
        per_device, mesh=fine, in_specs=in_specs, out_specs=out_specs, check_vma=False
    )
```

```python
import jax
import jax.numpy as jnp
import numpy as np
from jax import lax
from jax.sharding import Mesh
from jax.sharding import PartitionSpec as P

D = 6144
HEAD_SIZE = 128
EXPERTS = 4
CAP = 32
EPS = 1e-05

CTX = ("zl", "core")
REQ = ("y", "x", "zh")
Z_AXES = ("zl", "zh")


def route_tables(expert_ids, gate_num):
    blocks = expert_ids.shape[0]
    per_block = expert_ids.shape[1]
    top_k = expert_ids.shape[2]
    flat_ids = expert_ids.reshape(blocks, per_block * top_k)
    onehot = (flat_ids[..., None] == jnp.arange(EXPERTS, dtype=jnp.int32)).astype(jnp.int32)
    before = jnp.cumsum(onehot, axis=1) - onehot
    slot_num = jnp.sum(onehot * before, axis=-1)
    target = flat_ids * CAP + slot_num
    one_table = (target[..., None] == jnp.arange(EXPERTS * CAP, dtype=jnp.int32)).astype(
        jnp.float32
    )
    one_table = one_table.reshape(blocks, per_block, top_k, EXPERTS * CAP)
    fractions = gate_num.astype(jnp.float32) / 256.0
    dispatch = jnp.sum(one_table, axis=2)
    combine = jnp.sum(one_table * fractions[..., None], axis=2)
    return (dispatch, combine)


def attend_part(query_row_block, query_slot, key_row_block, value_row_block, key_slot):
    query_count = query_row_block.shape[0]
    key_count = key_row_block.shape[0]
    n_kv = key_row_block.shape[1] // HEAD_SIZE
    query_groups = query_row_block.shape[1] // HEAD_SIZE // n_kv
    query_head_rows = query_row_block.reshape(query_count, n_kv, query_groups, HEAD_SIZE)
    key_head_rows = key_row_block.reshape(key_count, n_kv, HEAD_SIZE)
    value_head_rows = value_row_block.reshape(key_count, n_kv, HEAD_SIZE)
    scores = jnp.einsum(
        "qhgd,khd->hgqk", query_head_rows, key_head_rows, preferred_element_type=jnp.float32
    ) * HEAD_SIZE ** (-0.5)
    capped = 30.0 * jnp.tanh(scores / 30.0)
    visible = key_slot[None, None, None, :] <= query_slot[None, None, :, None]
    attn_weights = jnp.where(visible, jnp.exp(capped), 0.0).astype(jnp.bfloat16)
    totals = jnp.sum(attn_weights.astype(jnp.float32), axis=-1)
    totals = jnp.transpose(totals, (2, 0, 1)).reshape(query_count, n_kv * query_groups)
    numerator = jnp.einsum(
        "hgqk,khd->qhgd", attn_weights, value_head_rows, preferred_element_type=jnp.float32
    )
    return (numerator.reshape(query_count, n_kv * query_groups * HEAD_SIZE), totals)


def col_slice(values, width):
    start = lax.axis_index(CTX) * width
    return lax.dynamic_slice_in_dim(values, start, width, values.ndim - 1)


def row_scale(local_rows, gain_cols):
    sum_sq = lax.psum(jnp.sum(local_rows * local_rows, axis=-1, keepdims=True), "core")
    sum_sq = lax.psum(sum_sq, "zl")
    return local_rows * lax.rsqrt(sum_sq / D + EPS) * gain_cols


def ring_perms(n, place):
    fwd = [(place[i], place[(i + 1) % n]) for i in range(n)]
    bwd = [(place[i], place[(i - 1) % n]) for i in range(n)]
    return fwd, bwd


def ring_gather(block, axis, n, place):
    fwd, bwd = ring_perms(n, place)
    half = block.shape[0] // 2
    out = [None] * n
    out[0] = block
    from_prev = block
    from_next = block
    for d in range(1, n // 2 + 1):
        if 2 * d == n:
            out[d] = jnp.concatenate(
                [
                    lax.ppermute(from_prev[:half], axis, fwd),
                    lax.ppermute(from_next[half:], axis, bwd),
                ]
            )
        else:
            from_prev = lax.ppermute(from_prev, axis, fwd)
            from_next = lax.ppermute(from_next, axis, bwd)
            out[n - d] = from_prev
            out[d] = from_next
    return out


def ring_reduce(parts, axis, n, place):
    fwd, bwd = ring_perms(n, place)
    far = n // 2
    half = parts[0].shape[0] // 2
    got_prev = lax.ppermute(parts[far][:half].astype(jnp.bfloat16), axis, fwd)
    got_next = lax.ppermute(parts[far][half:].astype(jnp.bfloat16), axis, bwd)
    pad = jnp.zeros_like(got_prev)
    got_prev = jnp.concatenate([got_prev, pad])
    got_next = jnp.concatenate([pad, got_next])
    for d in range(far - 1, 0, -1):
        send_next = (parts[d] + got_prev.astype(jnp.float32)).astype(jnp.bfloat16)
        send_prev = (parts[n - d] + got_next.astype(jnp.float32)).astype(jnp.bfloat16)
        got_prev = lax.ppermute(send_next, axis, fwd)
        got_next = lax.ppermute(send_prev, axis, bwd)
    return parts[0] + got_prev.astype(jnp.float32) + got_next.astype(jnp.float32)


def per_device(
    queries,
    cached_keys,
    cached_values,
    fresh_keys,
    fresh_values,
    slot_order,
    residual,
    expert_ids,
    gate_num,
    gain_attn,
    gain_pre,
    gain_post,
    w_gate,
    w_up,
    w_down,
):
    query_row_block = queries[0]
    query_count = query_row_block.shape[0]
    width = query_row_block.shape[1]
    query_slot = slot_order[0].astype(jnp.float32)
    head_width = fresh_keys.shape[2]
    n_ctx = D // width

    with jax.named_scope("attention"):
        new_numer, new_totals = attend_part(
            query_row_block, query_slot, fresh_keys[0], fresh_values[0], query_slot
        )
        cache_rows = cached_keys.shape[1]
        both_heads = jnp.stack([cached_keys[0], cached_values[0]]).reshape(
            2, cache_rows, n_ctx, head_width
        )
        both_part = lax.all_to_all(both_heads, CTX, split_axis=2, concat_axis=1, tiled=True)
        key_part = both_part[0].reshape(-1, head_width)
        value_part = both_part[1].reshape(-1, head_width)
        cache_slot = jnp.full((key_part.shape[0],), -1.0, jnp.float32)
        numer_part, total_part = attend_part(
            query_row_block, query_slot, key_part, value_part, cache_slot
        )
        numerator = new_numer + numer_part
        totals = new_totals + total_part
        local_heads = (
            numerator.reshape(query_count, -1, HEAD_SIZE) / totals[..., None]
        ).reshape(query_count, -1)

    with jax.named_scope("norms"):
        residual_cols = col_slice(residual[0], width).astype(jnp.float32)
        hidden_cols = (residual_cols + row_scale(local_heads, col_slice(gain_attn, width))).astype(
            jnp.bfloat16
        )
        normed_cols = row_scale(hidden_cols.astype(jnp.float32), col_slice(gain_pre, width)).astype(
            jnp.bfloat16
        )

    dispatch, combine = route_tables(expert_ids, gate_num)
    n_zl = D // width // 2
    group = CAP // n_zl
    swap = [(0, 1), (1, 0)]
    with jax.named_scope("dispatch"):
        buffer = jnp.einsum(
            "ns,nd->sd",
            dispatch[0].astype(jnp.bfloat16),
            normed_cols,
            preferred_element_type=jnp.float32,
        ).astype(jnp.bfloat16)
        rows = buffer.reshape(EXPERTS * n_zl, group, width)
        rows = lax.all_to_all(rows, ("y", "zl"), split_axis=0, concat_axis=0, tiled=True)
        rows = jnp.transpose(rows.reshape(EXPERTS, n_zl, group, width), (0, 2, 1, 3))
        n_x = lax.axis_size("x")
        n_z = 2 * n_zl
        z_place = [(z % n_zl) * 2 + z // n_zl for z in range(n_z)]
        x_place = list(range(n_x))
        z_blocks = ring_gather(rows.reshape(-1, n_zl * width), Z_AXES, n_z, z_place)
        block = jnp.concatenate(z_blocks)
        own_blocks = ring_gather(block, "x", n_x, x_place)

    with jax.named_scope("experts"):
        core = lax.axis_index("core")

        def halves(mat, axis):
            shape = mat.shape
            split = shape[:axis] + (n_zl, 2, width) + shape[axis + 1 :]
            mat = mat.reshape(split)
            own = lax.dynamic_index_in_dim(mat, core, axis + 1, keepdims=False)
            other = lax.dynamic_index_in_dim(mat, 1 - core, axis + 1, keepdims=False)
            merged = shape[:axis] + (n_zl * width,) + shape[axis + 1 :]
            return own.reshape(merged), other.reshape(merged)

        gate_own, gate_other = halves(w_gate[0], 0)
        up_own, up_other = halves(w_up[0], 0)
        down_own, down_other = halves(w_down[0], 1)

        def expert_block(own_rows):
            other_rows = lax.ppermute(own_rows, "core", swap)
            pre_gate = jnp.dot(own_rows, gate_own, preferred_element_type=jnp.float32) + jnp.dot(
                other_rows, gate_other, preferred_element_type=jnp.float32
            )
            pre_up = jnp.dot(own_rows, up_own, preferred_element_type=jnp.float32) + jnp.dot(
                other_rows, up_other, preferred_element_type=jnp.float32
            )
            hidden_units = (jax.nn.gelu(pre_gate) * pre_up).astype(jnp.bfloat16)
            piece_own = jnp.dot(
                hidden_units, down_own, preferred_element_type=jnp.float32
            ).astype(jnp.bfloat16)
            piece_other = jnp.dot(
                hidden_units, down_other, preferred_element_type=jnp.float32
            ).astype(jnp.bfloat16)
            received = lax.ppermute(piece_other, "core", swap)
            return piece_own.astype(jnp.float32) + received.astype(jnp.float32)

        sums = [expert_block(b) for b in own_blocks]

    with jax.named_scope("combine"):
        x_sum = ring_reduce(sums, "x", n_x, x_place)
        z_parts = jnp.split(x_sum, n_z)
        parts = ring_reduce(z_parts, Z_AXES, n_z, z_place).astype(jnp.bfloat16)
        parts = jnp.transpose(parts.reshape(EXPERTS, group, n_zl, width), (0, 2, 1, 3))
        parts = parts.reshape(EXPERTS * n_zl, group, width)
        outs = lax.all_to_all(parts, ("y", "zl"), split_axis=0, concat_axis=0, tiled=True)
        expert_cols = outs.reshape(EXPERTS * CAP, width).astype(jnp.float32)
        mixture = jnp.dot(combine[0], expert_cols, precision=lax.Precision.HIGHEST)
        layer_cols = (
            hidden_cols.astype(jnp.float32) + row_scale(mixture, col_slice(gain_post, width))
        ).astype(jnp.bfloat16)
        layer_out = lax.all_gather(layer_cols, CTX, axis=1, tiled=True)
    return layer_out[None]


def solution(mesh):
    n_exp = mesh.shape["exp"]
    n_ctx = mesh.shape["ctx"]
    sizes = {"y": EXPERTS, "x": n_exp // EXPERTS // 2, "zh": 2, "zl": n_ctx // 2, "core": 2}
    parts = {"exp": ("y", "x", "zh"), "ctx": ("zl", "core")}
    names = tuple(n for axis in mesh.axis_names for n in parts[axis])
    devices = np.asarray(mesh.devices).reshape(tuple(sizes[n] for n in names))
    fine = Mesh(devices, names)
    in_specs = (
        P(REQ, None, CTX),
        P(REQ, CTX, None),
        P(REQ, CTX, None),
        P(REQ, None, CTX),
        P(REQ, None, CTX),
        P(REQ, None),
        P(REQ, None, None),
        P(REQ, None, None),
        P(REQ, None, None),
        P(),
        P(),
        P(),
        P(REQ, None, CTX),
        P(REQ, None, CTX),
        P(REQ, CTX, None),
    )
    out_specs = P(REQ, None, None)
    return jax.shard_map(
        per_device, mesh=fine, in_specs=in_specs, out_specs=out_specs, check_vma=False
    )
```

```python
import jax
import jax.numpy as jnp
import numpy as np
from jax import lax
from jax.sharding import Mesh
from jax.sharding import PartitionSpec as P

D = 6144
HEAD_SIZE = 128
EXPERTS = 4
CAP = 32
EPS = 1e-05

CTX = ("zl", "core")
REQ = ("y", "x", "zh")
Z_AXES = ("zl", "zh")


def route_tables(expert_ids, gate_num):
    blocks = expert_ids.shape[0]
    per_block = expert_ids.shape[1]
    top_k = expert_ids.shape[2]
    flat_ids = expert_ids.reshape(blocks, per_block * top_k)
    onehot = (flat_ids[..., None] == jnp.arange(EXPERTS, dtype=jnp.int32)).astype(jnp.int32)
    before = jnp.cumsum(onehot, axis=1) - onehot
    slot_num = jnp.sum(onehot * before, axis=-1)
    target = flat_ids * CAP + slot_num
    one_table = (target[..., None] == jnp.arange(EXPERTS * CAP, dtype=jnp.int32)).astype(
        jnp.float32
    )
    one_table = one_table.reshape(blocks, per_block, top_k, EXPERTS * CAP)
    fractions = gate_num.astype(jnp.float32) / 256.0
    dispatch = jnp.sum(one_table, axis=2)
    combine = jnp.sum(one_table * fractions[..., None], axis=2)
    return (dispatch, combine)


def attend_part(query_row_block, query_slot, key_row_block, value_row_block, key_slot):
    query_count = query_row_block.shape[0]
    key_count = key_row_block.shape[0]
    n_kv = key_row_block.shape[1] // HEAD_SIZE
    query_groups = query_row_block.shape[1] // HEAD_SIZE // n_kv
    query_head_rows = query_row_block.reshape(query_count, n_kv, query_groups, HEAD_SIZE)
    key_head_rows = key_row_block.reshape(key_count, n_kv, HEAD_SIZE)
    value_head_rows = value_row_block.reshape(key_count, n_kv, HEAD_SIZE)
    scores = jnp.einsum(
        "qhgd,khd->hgqk", query_head_rows, key_head_rows, preferred_element_type=jnp.float32
    ) * HEAD_SIZE ** (-0.5)
    capped = 30.0 * jnp.tanh(scores / 30.0)
    visible = key_slot[None, None, None, :] <= query_slot[None, None, :, None]
    attn_weights = jnp.where(visible, jnp.exp(capped), 0.0).astype(jnp.bfloat16)
    totals = jnp.sum(attn_weights.astype(jnp.float32), axis=-1)
    totals = jnp.transpose(totals, (2, 0, 1)).reshape(query_count, n_kv * query_groups)
    numerator = jnp.einsum(
        "hgqk,khd->qhgd", attn_weights, value_head_rows, preferred_element_type=jnp.float32
    )
    return (numerator.reshape(query_count, n_kv * query_groups * HEAD_SIZE), totals)


def col_slice(values, width):
    start = lax.axis_index(CTX) * width
    return lax.dynamic_slice_in_dim(values, start, width, values.ndim - 1)


def row_scale(local_rows, gain_cols):
    sum_sq = lax.psum(jnp.sum(local_rows * local_rows, axis=-1, keepdims=True), "core")
    sum_sq = lax.psum(sum_sq, "zl")
    return local_rows * lax.rsqrt(sum_sq / D + EPS) * gain_cols


def ring_perms(n, place):
    fwd = [(place[i], place[(i + 1) % n]) for i in range(n)]
    bwd = [(place[i], place[(i - 1) % n]) for i in range(n)]
    return fwd, bwd


def ring_gather(block, axis, n, place):
    fwd, bwd = ring_perms(n, place)
    half = block.shape[0] // 2
    out = [None] * n
    out[0] = block
    from_prev = block
    from_next = block
    for d in range(1, n // 2 + 1):
        if 2 * d == n:
            out[d] = jnp.concatenate(
                [
                    lax.ppermute(from_prev[:half], axis, fwd),
                    lax.ppermute(from_next[half:], axis, bwd),
                ]
            )
        else:
            from_prev = lax.ppermute(from_prev, axis, fwd)
            from_next = lax.ppermute(from_next, axis, bwd)
            out[n - d] = from_prev
            out[d] = from_next
    return out


def ring_reduce(parts, axis, n, place):
    fwd, bwd = ring_perms(n, place)
    far = n // 2
    half = parts[0].shape[0] // 2
    got_prev = lax.ppermute(parts[far][:half].astype(jnp.bfloat16), axis, fwd)
    got_next = lax.ppermute(parts[far][half:].astype(jnp.bfloat16), axis, bwd)
    pad = jnp.zeros_like(got_prev)
    got_prev = jnp.concatenate([got_prev, pad])
    got_next = jnp.concatenate([pad, got_next])
    for d in range(far - 1, 0, -1):
        send_next = (parts[d] + got_prev.astype(jnp.float32)).astype(jnp.bfloat16)
        send_prev = (parts[n - d] + got_next.astype(jnp.float32)).astype(jnp.bfloat16)
        got_prev = lax.ppermute(send_next, axis, fwd)
        got_next = lax.ppermute(send_prev, axis, bwd)
    return parts[0] + got_prev.astype(jnp.float32) + got_next.astype(jnp.float32)


def per_device(
    queries,
    cached_keys,
    cached_values,
    fresh_keys,
    fresh_values,
    slot_order,
    residual,
    expert_ids,
    gate_num,
    gain_attn,
    gain_pre,
    gain_post,
    w_gate,
    w_up,
    w_down,
):
    query_row_block = queries[0]
    query_count = query_row_block.shape[0]
    width = query_row_block.shape[1]
    query_slot = slot_order[0].astype(jnp.float32)
    head_width = fresh_keys.shape[2]
    n_ctx = D // width

    with jax.named_scope("attention"):
        new_numer, new_totals = attend_part(
            query_row_block, query_slot, fresh_keys[0], fresh_values[0], query_slot
        )
        cache_rows = cached_keys.shape[1]
        both_heads = jnp.stack([cached_keys[0], cached_values[0]]).reshape(
            2, cache_rows, n_ctx, head_width
        )
        both_part = lax.all_to_all(both_heads, CTX, split_axis=2, concat_axis=1, tiled=True)
        key_part = both_part[0].reshape(-1, head_width)
        value_part = both_part[1].reshape(-1, head_width)
        cache_slot = jnp.full((key_part.shape[0],), -1.0, jnp.float32)
        numer_part, total_part = attend_part(
            query_row_block, query_slot, key_part, value_part, cache_slot
        )
        numerator = new_numer + numer_part
        totals = new_totals + total_part
        local_heads = (
            numerator.reshape(query_count, -1, HEAD_SIZE) / totals[..., None]
        ).reshape(query_count, -1)

    with jax.named_scope("norms"):
        residual_cols = col_slice(residual[0], width).astype(jnp.float32)
        hidden_cols = (residual_cols + row_scale(local_heads, col_slice(gain_attn, width))).astype(
            jnp.bfloat16
        )
        normed_cols = row_scale(hidden_cols.astype(jnp.float32), col_slice(gain_pre, width)).astype(
            jnp.bfloat16
        )

    dispatch, combine = route_tables(expert_ids, gate_num)
    n_zl = D // width // 2
    group = CAP // n_zl
    swap = [(0, 1), (1, 0)]
    with jax.named_scope("dispatch"):
        buffer = jnp.einsum(
            "ns,nd->sd",
            dispatch[0].astype(jnp.bfloat16),
            normed_cols,
            preferred_element_type=jnp.float32,
        ).astype(jnp.bfloat16)
        rows = buffer.reshape(EXPERTS * n_zl, group, width)
        rows = lax.all_to_all(rows, ("y", "zl"), split_axis=0, concat_axis=0, tiled=True)
        rows = jnp.transpose(rows.reshape(EXPERTS, n_zl, group, width), (0, 2, 1, 3))
        n_x = lax.axis_size("x")
        n_z = 2 * n_zl
        z_place = [(z % n_zl) * 2 + z // n_zl for z in range(n_z)]
        x_place = list(range(n_x))
        z_blocks = ring_gather(rows.reshape(-1, n_zl * width), Z_AXES, n_z, z_place)
        block = jnp.concatenate(z_blocks)
        own_blocks = ring_gather(block, "x", n_x, x_place)

    with jax.named_scope("experts"):
        core = lax.axis_index("core")

        def halves(mat, axis):
            shape = mat.shape
            split = shape[:axis] + (n_zl, 2, width) + shape[axis + 1 :]
            mat = mat.reshape(split)
            own = lax.dynamic_index_in_dim(mat, core, axis + 1, keepdims=False)
            other = lax.dynamic_index_in_dim(mat, 1 - core, axis + 1, keepdims=False)
            merged = shape[:axis] + (n_zl * width,) + shape[axis + 1 :]
            return own.reshape(merged), other.reshape(merged)

        gate_own, gate_other = halves(w_gate[0], 0)
        up_own, up_other = halves(w_up[0], 0)
        down_own, down_other = halves(w_down[0], 1)

        def expert_block(own_rows):
            other_rows = lax.ppermute(own_rows, "core", swap)
            pre_gate = jnp.dot(own_rows, gate_own, preferred_element_type=jnp.float32) + jnp.dot(
                other_rows, gate_other, preferred_element_type=jnp.float32
            )
            pre_up = jnp.dot(own_rows, up_own, preferred_element_type=jnp.float32) + jnp.dot(
                other_rows, up_other, preferred_element_type=jnp.float32
            )
            hidden_units = (jax.nn.gelu(pre_gate) * pre_up).astype(jnp.bfloat16)
            piece_own = jnp.dot(
                hidden_units, down_own, preferred_element_type=jnp.float32
            ).astype(jnp.bfloat16)
            piece_other = jnp.dot(
                hidden_units, down_other, preferred_element_type=jnp.float32
            ).astype(jnp.bfloat16)
            received = lax.ppermute(piece_other, "core", swap)
            return piece_own.astype(jnp.float32) + received.astype(jnp.float32)

        sums = [expert_block(b) for b in own_blocks]

    with jax.named_scope("combine"):
        x_sum = ring_reduce(sums, "x", n_x, x_place)
        z_parts = jnp.split(x_sum, n_z)
        parts = ring_reduce(z_parts, Z_AXES, n_z, z_place).astype(jnp.bfloat16)
        parts = jnp.transpose(parts.reshape(EXPERTS, group, n_zl, width), (0, 2, 1, 3))
        parts = parts.reshape(EXPERTS * n_zl, group, width)
        outs = lax.all_to_all(parts, ("y", "zl"), split_axis=0, concat_axis=0, tiled=True)
        expert_cols = outs.reshape(EXPERTS * CAP, width).astype(jnp.float32)
        mixture = jnp.dot(combine[0], expert_cols, precision=lax.Precision.HIGHEST)
        layer_cols = (
            hidden_cols.astype(jnp.float32) + row_scale(mixture, col_slice(gain_post, width))
        ).astype(jnp.bfloat16)
        layer_out = lax.all_gather(layer_cols, "core", axis=1, tiled=True)
        layer_out = lax.all_gather(layer_out, "zl", axis=1, tiled=True)
    return layer_out[None]


def solution(mesh):
    n_exp = mesh.shape["exp"]
    n_ctx = mesh.shape["ctx"]
    sizes = {"y": EXPERTS, "x": n_exp // EXPERTS // 2, "zh": 2, "zl": n_ctx // 2, "core": 2}
    parts = {"exp": ("y", "x", "zh"), "ctx": ("zl", "core")}
    names = tuple(n for axis in mesh.axis_names for n in parts[axis])
    devices = np.asarray(mesh.devices).reshape(tuple(sizes[n] for n in names))
    fine = Mesh(devices, names)
    in_specs = (
        P(REQ, None, CTX),
        P(REQ, CTX, None),
        P(REQ, CTX, None),
        P(REQ, None, CTX),
        P(REQ, None, CTX),
        P(REQ, None),
        P(REQ, None, None),
        P(REQ, None, None),
        P(REQ, None, None),
        P(),
        P(),
        P(),
        P(REQ, None, CTX),
        P(REQ, None, CTX),
        P(REQ, CTX, None),
    )
    out_specs = P(REQ, None, None)
    return jax.shard_map(
        per_device, mesh=fine, in_specs=in_specs, out_specs=out_specs, check_vma=False
    )
```

```python
import jax
import jax.numpy as jnp
import numpy as np
from jax import lax
from jax.sharding import Mesh
from jax.sharding import PartitionSpec as P

D = 6144
HEAD_SIZE = 128
EXPERTS = 4
CAP = 32
EPS = 1e-05

CTX = ("zl", "core")
REQ = ("y", "x", "zh")
Z_AXES = ("zl", "zh")


def route_tables(expert_ids, gate_num):
    blocks = expert_ids.shape[0]
    per_block = expert_ids.shape[1]
    top_k = expert_ids.shape[2]
    flat_ids = expert_ids.reshape(blocks, per_block * top_k)
    onehot = (flat_ids[..., None] == jnp.arange(EXPERTS, dtype=jnp.int32)).astype(jnp.int32)
    before = jnp.cumsum(onehot, axis=1) - onehot
    slot_num = jnp.sum(onehot * before, axis=-1)
    target = flat_ids * CAP + slot_num
    one_table = (target[..., None] == jnp.arange(EXPERTS * CAP, dtype=jnp.int32)).astype(
        jnp.float32
    )
    one_table = one_table.reshape(blocks, per_block, top_k, EXPERTS * CAP)
    fractions = gate_num.astype(jnp.float32) / 256.0
    dispatch = jnp.sum(one_table, axis=2)
    combine = jnp.sum(one_table * fractions[..., None], axis=2)
    return (dispatch, combine)


def attend_part(query_row_block, query_slot, key_row_block, value_row_block, key_slot):
    query_count = query_row_block.shape[0]
    key_count = key_row_block.shape[0]
    n_kv = key_row_block.shape[1] // HEAD_SIZE
    query_groups = query_row_block.shape[1] // HEAD_SIZE // n_kv
    query_head_rows = query_row_block.reshape(query_count, n_kv, query_groups, HEAD_SIZE)
    key_head_rows = key_row_block.reshape(key_count, n_kv, HEAD_SIZE)
    value_head_rows = value_row_block.reshape(key_count, n_kv, HEAD_SIZE)
    scores = jnp.einsum(
        "qhgd,khd->hgqk", query_head_rows, key_head_rows, preferred_element_type=jnp.float32
    ) * HEAD_SIZE ** (-0.5)
    capped = 30.0 * jnp.tanh(scores / 30.0)
    visible = key_slot[None, None, None, :] <= query_slot[None, None, :, None]
    attn_weights = jnp.where(visible, jnp.exp(capped), 0.0).astype(jnp.bfloat16)
    totals = jnp.sum(attn_weights.astype(jnp.float32), axis=-1)
    totals = jnp.transpose(totals, (2, 0, 1)).reshape(query_count, n_kv * query_groups)
    numerator = jnp.einsum(
        "hgqk,khd->qhgd", attn_weights, value_head_rows, preferred_element_type=jnp.float32
    )
    return (numerator.reshape(query_count, n_kv * query_groups * HEAD_SIZE), totals)


def col_slice(values, width):
    start = lax.axis_index(CTX) * width
    return lax.dynamic_slice_in_dim(values, start, width, values.ndim - 1)


def row_scale(local_rows, gain_cols):
    sum_sq = lax.psum(jnp.sum(local_rows * local_rows, axis=-1, keepdims=True), "core")
    sum_sq = lax.psum(sum_sq, "zl")
    return local_rows * lax.rsqrt(sum_sq / D + EPS) * gain_cols


def ring_perms(n, place):
    fwd = [(place[i], place[(i + 1) % n]) for i in range(n)]
    bwd = [(place[i], place[(i - 1) % n]) for i in range(n)]
    return fwd, bwd


def ring_gather(block, axis, n, place):
    fwd, bwd = ring_perms(n, place)
    half = block.shape[0] // 2
    out = [None] * n
    out[0] = block
    from_prev = block
    from_next = block
    for d in range(1, n // 2 + 1):
        if 2 * d == n:
            out[d] = jnp.concatenate(
                [
                    lax.ppermute(from_prev[:half], axis, fwd),
                    lax.ppermute(from_next[half:], axis, bwd),
                ]
            )
        else:
            from_prev = lax.ppermute(from_prev, axis, fwd)
            from_next = lax.ppermute(from_next, axis, bwd)
            out[n - d] = from_prev
            out[d] = from_next
    return out


def ring_reduce(parts, axis, n, place):
    fwd, bwd = ring_perms(n, place)
    far = n // 2
    half = parts[0].shape[0] // 2
    got_prev = lax.ppermute(parts[far][:half].astype(jnp.bfloat16), axis, fwd)
    got_next = lax.ppermute(parts[far][half:].astype(jnp.bfloat16), axis, bwd)
    pad = jnp.zeros_like(got_prev)
    got_prev = jnp.concatenate([got_prev, pad])
    got_next = jnp.concatenate([pad, got_next])
    for d in range(far - 1, 0, -1):
        send_next = (parts[d] + got_prev.astype(jnp.float32)).astype(jnp.bfloat16)
        send_prev = (parts[n - d] + got_next.astype(jnp.float32)).astype(jnp.bfloat16)
        got_prev = lax.ppermute(send_next, axis, fwd)
        got_next = lax.ppermute(send_prev, axis, bwd)
    return parts[0] + got_prev.astype(jnp.float32) + got_next.astype(jnp.float32)


def per_device(
    queries,
    cached_keys,
    cached_values,
    fresh_keys,
    fresh_values,
    slot_order,
    residual,
    expert_ids,
    gate_num,
    gain_attn,
    gain_pre,
    gain_post,
    w_gate,
    w_up,
    w_down,
):
    query_row_block = queries[0]
    query_count = query_row_block.shape[0]
    width = query_row_block.shape[1]
    query_slot = slot_order[0].astype(jnp.float32)
    head_width = fresh_keys.shape[2]
    n_ctx = D // width

    with jax.named_scope("attention"):
        new_numer, new_totals = attend_part(
            query_row_block, query_slot, fresh_keys[0], fresh_values[0], query_slot
        )
        cache_rows = cached_keys.shape[1]
        both_heads = jnp.stack([cached_keys[0], cached_values[0]]).reshape(
            2, cache_rows, n_ctx, head_width
        )
        both_part = lax.all_to_all(both_heads, "zl", split_axis=2, concat_axis=1, tiled=True)
        both_part = lax.all_to_all(both_part, "core", split_axis=2, concat_axis=1, tiled=True)
        key_part = both_part[0].reshape(-1, head_width)
        value_part = both_part[1].reshape(-1, head_width)
        cache_slot = jnp.full((key_part.shape[0],), -1.0, jnp.float32)
        numer_part, total_part = attend_part(
            query_row_block, query_slot, key_part, value_part, cache_slot
        )
        numerator = new_numer + numer_part
        totals = new_totals + total_part
        local_heads = (
            numerator.reshape(query_count, -1, HEAD_SIZE) / totals[..., None]
        ).reshape(query_count, -1)

    with jax.named_scope("norms"):
        residual_cols = col_slice(residual[0], width).astype(jnp.float32)
        hidden_cols = (residual_cols + row_scale(local_heads, col_slice(gain_attn, width))).astype(
            jnp.bfloat16
        )
        normed_cols = row_scale(hidden_cols.astype(jnp.float32), col_slice(gain_pre, width)).astype(
            jnp.bfloat16
        )

    dispatch, combine = route_tables(expert_ids, gate_num)
    n_zl = D // width // 2
    group = CAP // n_zl
    swap = [(0, 1), (1, 0)]
    with jax.named_scope("dispatch"):
        buffer = jnp.einsum(
            "ns,nd->sd",
            dispatch[0].astype(jnp.bfloat16),
            normed_cols,
            preferred_element_type=jnp.float32,
        ).astype(jnp.bfloat16)
        rows = buffer.reshape(EXPERTS * n_zl, group, width)
        rows = lax.all_to_all(rows, ("y", "zl"), split_axis=0, concat_axis=0, tiled=True)
        rows = jnp.transpose(rows.reshape(EXPERTS, n_zl, group, width), (0, 2, 1, 3))
        n_x = lax.axis_size("x")
        n_z = 2 * n_zl
        z_place = [(z % n_zl) * 2 + z // n_zl for z in range(n_z)]
        x_place = list(range(n_x))
        z_blocks = ring_gather(rows.reshape(-1, n_zl * width), Z_AXES, n_z, z_place)
        block = jnp.concatenate(z_blocks)
        own_blocks = ring_gather(block, "x", n_x, x_place)

    with jax.named_scope("experts"):
        core = lax.axis_index("core")

        def halves(mat, axis):
            shape = mat.shape
            split = shape[:axis] + (n_zl, 2, width) + shape[axis + 1 :]
            mat = mat.reshape(split)
            own = lax.dynamic_index_in_dim(mat, core, axis + 1, keepdims=False)
            other = lax.dynamic_index_in_dim(mat, 1 - core, axis + 1, keepdims=False)
            merged = shape[:axis] + (n_zl * width,) + shape[axis + 1 :]
            return own.reshape(merged), other.reshape(merged)

        gate_own, gate_other = halves(w_gate[0], 0)
        up_own, up_other = halves(w_up[0], 0)
        down_own, down_other = halves(w_down[0], 1)

        def expert_block(own_rows):
            other_rows = lax.ppermute(own_rows, "core", swap)
            pre_gate = jnp.dot(own_rows, gate_own, preferred_element_type=jnp.float32) + jnp.dot(
                other_rows, gate_other, preferred_element_type=jnp.float32
            )
            pre_up = jnp.dot(own_rows, up_own, preferred_element_type=jnp.float32) + jnp.dot(
                other_rows, up_other, preferred_element_type=jnp.float32
            )
            hidden_units = (jax.nn.gelu(pre_gate) * pre_up).astype(jnp.bfloat16)
            piece_own = jnp.dot(
                hidden_units, down_own, preferred_element_type=jnp.float32
            ).astype(jnp.bfloat16)
            piece_other = jnp.dot(
                hidden_units, down_other, preferred_element_type=jnp.float32
            ).astype(jnp.bfloat16)
            received = lax.ppermute(piece_other, "core", swap)
            return piece_own.astype(jnp.float32) + received.astype(jnp.float32)

        sums = [expert_block(b) for b in own_blocks]

    with jax.named_scope("combine"):
        x_sum = ring_reduce(sums, "x", n_x, x_place)
        z_parts = jnp.split(x_sum, n_z)
        parts = ring_reduce(z_parts, Z_AXES, n_z, z_place).astype(jnp.bfloat16)
        parts = jnp.transpose(parts.reshape(EXPERTS, group, n_zl, width), (0, 2, 1, 3))
        parts = parts.reshape(EXPERTS * n_zl, group, width)
        outs = lax.all_to_all(parts, ("y", "zl"), split_axis=0, concat_axis=0, tiled=True)
        expert_cols = outs.reshape(EXPERTS * CAP, width).astype(jnp.float32)
        mixture = jnp.dot(combine[0], expert_cols, precision=lax.Precision.HIGHEST)
        layer_cols = (
            hidden_cols.astype(jnp.float32) + row_scale(mixture, col_slice(gain_post, width))
        ).astype(jnp.bfloat16)
        layer_out = lax.all_gather(layer_cols, CTX, axis=1, tiled=True)
    return layer_out[None]


def solution(mesh):
    n_exp = mesh.shape["exp"]
    n_ctx = mesh.shape["ctx"]
    sizes = {"y": EXPERTS, "x": n_exp // EXPERTS // 2, "zh": 2, "zl": n_ctx // 2, "core": 2}
    parts = {"exp": ("y", "x", "zh"), "ctx": ("zl", "core")}
    names = tuple(n for axis in mesh.axis_names for n in parts[axis])
    devices = np.asarray(mesh.devices).reshape(tuple(sizes[n] for n in names))
    fine = Mesh(devices, names)
    in_specs = (
        P(REQ, None, CTX),
        P(REQ, CTX, None),
        P(REQ, CTX, None),
        P(REQ, None, CTX),
        P(REQ, None, CTX),
        P(REQ, None),
        P(REQ, None, None),
        P(REQ, None, None),
        P(REQ, None, None),
        P(),
        P(),
        P(),
        P(REQ, None, CTX),
        P(REQ, None, CTX),
        P(REQ, CTX, None),
    )
    out_specs = P(REQ, None, None)
    return jax.shard_map(
        per_device, mesh=fine, in_specs=in_specs, out_specs=out_specs, check_vma=False
    )
```

```python
import jax
import jax.numpy as jnp
import numpy as np
from jax import lax
from jax.sharding import Mesh
from jax.sharding import PartitionSpec as P

D = 6144
HEAD_SIZE = 128
EXPERTS = 4
CAP = 32
EPS = 1e-05

CTX = ("zl", "core")
REQ = ("y", "x", "zh")
Z_AXES = ("zl", "zh")


def route_tables(expert_ids, gate_num):
    blocks = expert_ids.shape[0]
    per_block = expert_ids.shape[1]
    top_k = expert_ids.shape[2]
    flat_ids = expert_ids.reshape(blocks, per_block * top_k)
    onehot = (flat_ids[..., None] == jnp.arange(EXPERTS, dtype=jnp.int32)).astype(jnp.int32)
    before = jnp.cumsum(onehot, axis=1) - onehot
    slot_num = jnp.sum(onehot * before, axis=-1)
    target = flat_ids * CAP + slot_num
    one_table = (target[..., None] == jnp.arange(EXPERTS * CAP, dtype=jnp.int32)).astype(
        jnp.float32
    )
    one_table = one_table.reshape(blocks, per_block, top_k, EXPERTS * CAP)
    fractions = gate_num.astype(jnp.float32) / 256.0
    dispatch = jnp.sum(one_table, axis=2)
    combine = jnp.sum(one_table * fractions[..., None], axis=2)
    return (dispatch, combine)


def attend_part(query_row_block, query_slot, key_row_block, value_row_block, key_slot):
    query_count = query_row_block.shape[0]
    key_count = key_row_block.shape[0]
    n_kv = key_row_block.shape[1] // HEAD_SIZE
    query_groups = query_row_block.shape[1] // HEAD_SIZE // n_kv
    query_head_rows = query_row_block.reshape(query_count, n_kv, query_groups, HEAD_SIZE)
    key_head_rows = key_row_block.reshape(key_count, n_kv, HEAD_SIZE)
    value_head_rows = value_row_block.reshape(key_count, n_kv, HEAD_SIZE)
    scores = jnp.einsum(
        "qhgd,khd->hgqk", query_head_rows, key_head_rows, preferred_element_type=jnp.float32
    ) * HEAD_SIZE ** (-0.5)
    capped = 30.0 * jnp.tanh(scores / 30.0)
    visible = key_slot[None, None, None, :] <= query_slot[None, None, :, None]
    attn_weights = jnp.where(visible, jnp.exp(capped), 0.0).astype(jnp.bfloat16)
    totals = jnp.sum(attn_weights.astype(jnp.float32), axis=-1)
    totals = jnp.transpose(totals, (2, 0, 1)).reshape(query_count, n_kv * query_groups)
    numerator = jnp.einsum(
        "hgqk,khd->qhgd", attn_weights, value_head_rows, preferred_element_type=jnp.float32
    )
    return (numerator.reshape(query_count, n_kv * query_groups * HEAD_SIZE), totals)


def col_slice(values, width):
    start = lax.axis_index(CTX) * width
    return lax.dynamic_slice_in_dim(values, start, width, values.ndim - 1)


def row_scale(local_rows, gain_cols):
    sum_sq = lax.psum(jnp.sum(local_rows * local_rows, axis=-1, keepdims=True), "core")
    sum_sq = lax.psum(sum_sq, "zl")
    return local_rows * lax.rsqrt(sum_sq / D + EPS) * gain_cols


def ring_perms(n, place):
    fwd = [(place[i], place[(i + 1) % n]) for i in range(n)]
    bwd = [(place[i], place[(i - 1) % n]) for i in range(n)]
    return fwd, bwd


def ring_gather(block, axis, n, place):
    fwd, bwd = ring_perms(n, place)
    half = block.shape[0] // 2
    out = [None] * n
    out[0] = block
    from_prev = block
    from_next = block
    for d in range(1, n // 2 + 1):
        if 2 * d == n:
            out[d] = jnp.concatenate(
                [
                    lax.ppermute(from_prev[:half], axis, fwd),
                    lax.ppermute(from_next[half:], axis, bwd),
                ]
            )
        else:
            from_prev = lax.ppermute(from_prev, axis, fwd)
            from_next = lax.ppermute(from_next, axis, bwd)
            out[n - d] = from_prev
            out[d] = from_next
    return out


def ring_reduce(parts, axis, n, place):
    fwd, bwd = ring_perms(n, place)
    far = n // 2
    half = parts[0].shape[0] // 2
    got_prev = lax.ppermute(parts[far][:half].astype(jnp.bfloat16), axis, fwd)
    got_next = lax.ppermute(parts[far][half:].astype(jnp.bfloat16), axis, bwd)
    pad = jnp.zeros_like(got_prev)
    got_prev = jnp.concatenate([got_prev, pad])
    got_next = jnp.concatenate([pad, got_next])
    for d in range(far - 1, 0, -1):
        send_next = (parts[d] + got_prev.astype(jnp.float32)).astype(jnp.bfloat16)
        send_prev = (parts[n - d] + got_next.astype(jnp.float32)).astype(jnp.bfloat16)
        got_prev = lax.ppermute(send_next, axis, fwd)
        got_next = lax.ppermute(send_prev, axis, bwd)
    return parts[0] + got_prev.astype(jnp.float32) + got_next.astype(jnp.float32)


def per_device(
    queries,
    cached_keys,
    cached_values,
    fresh_keys,
    fresh_values,
    slot_order,
    residual,
    expert_ids,
    gate_num,
    gain_attn,
    gain_pre,
    gain_post,
    w_gate,
    w_up,
    w_down,
):
    query_row_block = queries[0]
    query_count = query_row_block.shape[0]
    width = query_row_block.shape[1]
    query_slot = slot_order[0].astype(jnp.float32)
    head_width = fresh_keys.shape[2]
    n_ctx = D // width

    with jax.named_scope("attention"):
        cache_rows = cached_keys.shape[1]
        both_heads = jnp.stack([cached_keys[0], cached_values[0]]).reshape(
            2, cache_rows, n_ctx, head_width
        )
        both_part = lax.all_to_all(both_heads, CTX, split_axis=2, concat_axis=1, tiled=True)
        key_part = jnp.concatenate([both_part[0].reshape(-1, head_width), fresh_keys[0]])
        value_part = jnp.concatenate([both_part[1].reshape(-1, head_width), fresh_values[0]])
        cache_slot = jnp.full((key_part.shape[0] - query_count,), -1.0, jnp.float32)
        key_slot = jnp.concatenate([cache_slot, query_slot])
        numerator, totals = attend_part(query_row_block, query_slot, key_part, value_part, key_slot)
        local_heads = (
            numerator.reshape(query_count, -1, HEAD_SIZE) / totals[..., None]
        ).reshape(query_count, -1)

    with jax.named_scope("norms"):
        residual_cols = col_slice(residual[0], width).astype(jnp.float32)
        hidden_cols = (residual_cols + row_scale(local_heads, col_slice(gain_attn, width))).astype(
            jnp.bfloat16
        )
        normed_cols = row_scale(hidden_cols.astype(jnp.float32), col_slice(gain_pre, width)).astype(
            jnp.bfloat16
        )

    dispatch, combine = route_tables(expert_ids, gate_num)
    n_zl = D // width // 2
    group = CAP // n_zl
    swap = [(0, 1), (1, 0)]
    with jax.named_scope("dispatch"):
        buffer = jnp.einsum(
            "ns,nd->sd",
            dispatch[0].astype(jnp.bfloat16),
            normed_cols,
            preferred_element_type=jnp.float32,
        ).astype(jnp.bfloat16)
        rows = buffer.reshape(EXPERTS * n_zl, group, width)
        rows = lax.all_to_all(rows, ("y", "zl"), split_axis=0, concat_axis=0, tiled=True)
        rows = jnp.transpose(rows.reshape(EXPERTS, n_zl, group, width), (0, 2, 1, 3))
        n_x = lax.axis_size("x")
        n_z = 2 * n_zl
        z_place = [(z % n_zl) * 2 + z // n_zl for z in range(n_z)]
        x_place = list(range(n_x))
        z_blocks = ring_gather(rows.reshape(-1, n_zl * width), Z_AXES, n_z, z_place)
        block = jnp.concatenate(z_blocks)
        own_blocks = ring_gather(block, "x", n_x, x_place)

    with jax.named_scope("experts"):
        core = lax.axis_index("core")

        def halves(mat, axis):
            shape = mat.shape
            split = shape[:axis] + (n_zl, 2, width) + shape[axis + 1 :]
            mat = mat.reshape(split)
            own = lax.dynamic_index_in_dim(mat, core, axis + 1, keepdims=False)
            other = lax.dynamic_index_in_dim(mat, 1 - core, axis + 1, keepdims=False)
            merged = shape[:axis] + (n_zl * width,) + shape[axis + 1 :]
            return own.reshape(merged), other.reshape(merged)

        gate_own, gate_other = halves(w_gate[0], 0)
        up_own, up_other = halves(w_up[0], 0)
        down_own, down_other = halves(w_down[0], 1)

        def expert_block(own_rows):
            other_rows = lax.ppermute(own_rows, "core", swap)
            pre_gate = jnp.dot(own_rows, gate_own, preferred_element_type=jnp.float32) + jnp.dot(
                other_rows, gate_other, preferred_element_type=jnp.float32
            )
            pre_up = jnp.dot(own_rows, up_own, preferred_element_type=jnp.float32) + jnp.dot(
                other_rows, up_other, preferred_element_type=jnp.float32
            )
            hidden_units = (jax.nn.gelu(pre_gate) * pre_up).astype(jnp.bfloat16)
            piece_own = jnp.dot(
                hidden_units, down_own, preferred_element_type=jnp.float32
            ).astype(jnp.bfloat16)
            piece_other = jnp.dot(
                hidden_units, down_other, preferred_element_type=jnp.float32
            ).astype(jnp.bfloat16)
            received = lax.ppermute(piece_other, "core", swap)
            return piece_own.astype(jnp.float32) + received.astype(jnp.float32)

        sums = [expert_block(b) for b in own_blocks]

    with jax.named_scope("combine"):
        x_sum = ring_reduce(sums, "x", n_x, x_place)
        z_parts = jnp.split(x_sum, n_z)
        parts = ring_reduce(z_parts, Z_AXES, n_z, z_place).astype(jnp.bfloat16)
        parts = jnp.transpose(parts.reshape(EXPERTS, group, n_zl, width), (0, 2, 1, 3))
        parts = parts.reshape(EXPERTS * n_zl, group, width)
        outs = lax.all_to_all(parts, ("y", "zl"), split_axis=0, concat_axis=0, tiled=True)
        expert_cols = outs.reshape(EXPERTS * CAP, width).astype(jnp.float32)
        mixture = jnp.dot(combine[0], expert_cols, precision=lax.Precision.HIGHEST)
        layer_cols = (
            hidden_cols.astype(jnp.float32) + row_scale(mixture, col_slice(gain_post, width))
        ).astype(jnp.bfloat16)
        layer_out = lax.all_gather(layer_cols, CTX, axis=1, tiled=True)
    return layer_out[None]


def solution(mesh):
    n_exp = mesh.shape["exp"]
    n_ctx = mesh.shape["ctx"]
    sizes = {"y": EXPERTS, "x": n_exp // EXPERTS // 2, "zh": 2, "zl": n_ctx // 2, "core": 2}
    parts = {"exp": ("y", "x", "zh"), "ctx": ("zl", "core")}
    names = tuple(n for axis in mesh.axis_names for n in parts[axis])
    devices = np.asarray(mesh.devices).reshape(tuple(sizes[n] for n in names))
    fine = Mesh(devices, names)
    in_specs = (
        P(REQ, None, CTX),
        P(REQ, CTX, None),
        P(REQ, CTX, None),
        P(REQ, None, CTX),
        P(REQ, None, CTX),
        P(REQ, None),
        P(REQ, None, None),
        P(REQ, None, None),
        P(REQ, None, None),
        P(),
        P(),
        P(),
        P(REQ, None, CTX),
        P(REQ, None, CTX),
        P(REQ, CTX, None),
    )
    out_specs = P(REQ, None, None)
    return jax.shard_map(
        per_device, mesh=fine, in_specs=in_specs, out_specs=out_specs, check_vma=False
    )
```

```python
import jax
import jax.numpy as jnp
import numpy as np
from jax import lax
from jax.sharding import Mesh
from jax.sharding import PartitionSpec as P

D = 6144
HEAD_SIZE = 128
EXPERTS = 4
CAP = 32
EPS = 1e-05

CTX = ("zl", "core")
REQ = ("y", "x", "zh")
Z_AXES = ("zl", "zh")


def route_tables(expert_ids, gate_num):
    blocks = expert_ids.shape[0]
    per_block = expert_ids.shape[1]
    top_k = expert_ids.shape[2]
    flat_ids = expert_ids.reshape(blocks, per_block * top_k)
    onehot = (flat_ids[..., None] == jnp.arange(EXPERTS, dtype=jnp.int32)).astype(jnp.int32)
    before = jnp.cumsum(onehot, axis=1) - onehot
    slot_num = jnp.sum(onehot * before, axis=-1)
    target = flat_ids * CAP + slot_num
    one_table = (target[..., None] == jnp.arange(EXPERTS * CAP, dtype=jnp.int32)).astype(
        jnp.float32
    )
    one_table = one_table.reshape(blocks, per_block, top_k, EXPERTS * CAP)
    fractions = gate_num.astype(jnp.float32) / 256.0
    dispatch = jnp.sum(one_table, axis=2)
    combine = jnp.sum(one_table * fractions[..., None], axis=2)
    return (dispatch, combine)


def attend_part(query_row_block, query_slot, key_row_block, value_row_block, key_slot):
    query_count = query_row_block.shape[0]
    key_count = key_row_block.shape[0]
    n_kv = key_row_block.shape[1] // HEAD_SIZE
    query_groups = query_row_block.shape[1] // HEAD_SIZE // n_kv
    query_head_rows = query_row_block.reshape(query_count, n_kv, query_groups, HEAD_SIZE)
    key_head_rows = key_row_block.reshape(key_count, n_kv, HEAD_SIZE)
    value_head_rows = value_row_block.reshape(key_count, n_kv, HEAD_SIZE)
    scores = jnp.einsum(
        "qhgd,khd->hgqk", query_head_rows, key_head_rows, preferred_element_type=jnp.float32
    ) * HEAD_SIZE ** (-0.5)
    capped = 30.0 * jnp.tanh(scores / 30.0)
    visible = key_slot[None, None, None, :] <= query_slot[None, None, :, None]
    attn_weights = jnp.where(visible, jnp.exp(capped), 0.0).astype(jnp.bfloat16)
    totals = jnp.sum(attn_weights.astype(jnp.float32), axis=-1)
    totals = jnp.transpose(totals, (2, 0, 1)).reshape(query_count, n_kv * query_groups)
    numerator = jnp.einsum(
        "hgqk,khd->qhgd", attn_weights, value_head_rows, preferred_element_type=jnp.float32
    )
    return (numerator.reshape(query_count, n_kv * query_groups * HEAD_SIZE), totals)


def col_slice(values, width):
    start = lax.axis_index(CTX) * width
    return lax.dynamic_slice_in_dim(values, start, width, values.ndim - 1)


def row_scale(local_rows, gain_cols):
    sum_sq = lax.psum(jnp.sum(local_rows * local_rows, axis=-1, keepdims=True), "core")
    sum_sq = lax.psum(sum_sq, "zl")
    return local_rows * lax.rsqrt(sum_sq / D + EPS) * gain_cols


def ring_perms(n, place):
    fwd = [(place[i], place[(i + 1) % n]) for i in range(n)]
    bwd = [(place[i], place[(i - 1) % n]) for i in range(n)]
    return fwd, bwd


def ring_gather(block, axis, n, place):
    fwd, bwd = ring_perms(n, place)
    half = block.shape[0] // 2
    out = [None] * n
    out[0] = block
    from_prev = block
    from_next = block
    for d in range(1, n // 2 + 1):
        if 2 * d == n:
            out[d] = jnp.concatenate(
                [
                    lax.ppermute(from_prev[:half], axis, fwd),
                    lax.ppermute(from_next[half:], axis, bwd),
                ]
            )
        else:
            from_prev = lax.ppermute(from_prev, axis, fwd)
            from_next = lax.ppermute(from_next, axis, bwd)
            out[n - d] = from_prev
            out[d] = from_next
    return out


def ring_reduce(parts, axis, n, place):
    fwd, bwd = ring_perms(n, place)
    far = n // 2
    half = parts[0].shape[0] // 2
    got_prev = lax.ppermute(parts[far][:half].astype(jnp.bfloat16), axis, fwd)
    got_next = lax.ppermute(parts[far][half:].astype(jnp.bfloat16), axis, bwd)
    for d in range(far - 1, 0, -1):
        ahead = parts[d]
        behind = parts[n - d]
        if d == far - 1:
            ahead = ahead.at[:half].add(got_prev.astype(jnp.float32))
            behind = behind.at[half:].add(got_next.astype(jnp.float32))
        else:
            ahead = ahead + got_prev.astype(jnp.float32)
            behind = behind + got_next.astype(jnp.float32)
        send_next = ahead.astype(jnp.bfloat16)
        send_prev = behind.astype(jnp.bfloat16)
        got_prev = lax.ppermute(send_next, axis, fwd)
        got_next = lax.ppermute(send_prev, axis, bwd)
    return parts[0] + got_prev.astype(jnp.float32) + got_next.astype(jnp.float32)


def per_device(
    queries,
    cached_keys,
    cached_values,
    fresh_keys,
    fresh_values,
    slot_order,
    residual,
    expert_ids,
    gate_num,
    gain_attn,
    gain_pre,
    gain_post,
    w_gate,
    w_up,
    w_down,
):
    query_row_block = queries[0]
    query_count = query_row_block.shape[0]
    width = query_row_block.shape[1]
    query_slot = slot_order[0].astype(jnp.float32)
    head_width = fresh_keys.shape[2]
    n_ctx = D // width

    with jax.named_scope("attention"):
        new_numer, new_totals = attend_part(
            query_row_block, query_slot, fresh_keys[0], fresh_values[0], query_slot
        )
        cache_rows = cached_keys.shape[1]
        both_heads = jnp.stack([cached_keys[0], cached_values[0]]).reshape(
            2, cache_rows, n_ctx, head_width
        )
        both_part = lax.all_to_all(both_heads, CTX, split_axis=2, concat_axis=1, tiled=True)
        key_part = both_part[0].reshape(-1, head_width)
        value_part = both_part[1].reshape(-1, head_width)
        cache_slot = jnp.full((key_part.shape[0],), -1.0, jnp.float32)
        numer_part, total_part = attend_part(
            query_row_block, query_slot, key_part, value_part, cache_slot
        )
        numerator = new_numer + numer_part
        totals = new_totals + total_part
        local_heads = (
            numerator.reshape(query_count, -1, HEAD_SIZE) / totals[..., None]
        ).reshape(query_count, -1)

    with jax.named_scope("norms"):
        residual_cols = col_slice(residual[0], width).astype(jnp.float32)
        hidden_cols = (residual_cols + row_scale(local_heads, col_slice(gain_attn, width))).astype(
            jnp.bfloat16
        )
        normed_cols = row_scale(hidden_cols.astype(jnp.float32), col_slice(gain_pre, width)).astype(
            jnp.bfloat16
        )

    dispatch, combine = route_tables(expert_ids, gate_num)
    n_zl = D // width // 2
    group = CAP // n_zl
    swap = [(0, 1), (1, 0)]
    with jax.named_scope("dispatch"):
        buffer = jnp.einsum(
            "ns,nd->sd",
            dispatch[0].astype(jnp.bfloat16),
            normed_cols,
            preferred_element_type=jnp.float32,
        ).astype(jnp.bfloat16)
        rows = buffer.reshape(EXPERTS * n_zl, group, width)
        rows = lax.all_to_all(rows, ("y", "zl"), split_axis=0, concat_axis=0, tiled=True)
        rows = jnp.transpose(rows.reshape(EXPERTS, n_zl, group, width), (0, 2, 1, 3))
        n_x = lax.axis_size("x")
        n_z = 2 * n_zl
        z_place = [(z % n_zl) * 2 + z // n_zl for z in range(n_z)]
        x_place = list(range(n_x))
        z_blocks = ring_gather(rows.reshape(-1, n_zl * width), Z_AXES, n_z, z_place)
        block = jnp.concatenate(z_blocks)
        own_blocks = ring_gather(block, "x", n_x, x_place)

    with jax.named_scope("experts"):
        core = lax.axis_index("core")

        def halves(mat, axis):
            shape = mat.shape
            split = shape[:axis] + (n_zl, 2, width) + shape[axis + 1 :]
            mat = mat.reshape(split)
            own = lax.dynamic_index_in_dim(mat, core, axis + 1, keepdims=False)
            other = lax.dynamic_index_in_dim(mat, 1 - core, axis + 1, keepdims=False)
            merged = shape[:axis] + (n_zl * width,) + shape[axis + 1 :]
            return own.reshape(merged), other.reshape(merged)

        gate_own, gate_other = halves(w_gate[0], 0)
        up_own, up_other = halves(w_up[0], 0)
        down_own, down_other = halves(w_down[0], 1)

        def expert_block(own_rows):
            other_rows = lax.ppermute(own_rows, "core", swap)
            pre_gate = jnp.dot(own_rows, gate_own, preferred_element_type=jnp.float32) + jnp.dot(
                other_rows, gate_other, preferred_element_type=jnp.float32
            )
            pre_up = jnp.dot(own_rows, up_own, preferred_element_type=jnp.float32) + jnp.dot(
                other_rows, up_other, preferred_element_type=jnp.float32
            )
            hidden_units = (jax.nn.gelu(pre_gate) * pre_up).astype(jnp.bfloat16)
            piece_own = jnp.dot(
                hidden_units, down_own, preferred_element_type=jnp.float32
            ).astype(jnp.bfloat16)
            piece_other = jnp.dot(
                hidden_units, down_other, preferred_element_type=jnp.float32
            ).astype(jnp.bfloat16)
            received = lax.ppermute(piece_other, "core", swap)
            return piece_own.astype(jnp.float32) + received.astype(jnp.float32)

        sums = [expert_block(b) for b in own_blocks]

    with jax.named_scope("combine"):
        x_sum = ring_reduce(sums, "x", n_x, x_place)
        z_parts = jnp.split(x_sum, n_z)
        parts = ring_reduce(z_parts, Z_AXES, n_z, z_place).astype(jnp.bfloat16)
        parts = jnp.transpose(parts.reshape(EXPERTS, group, n_zl, width), (0, 2, 1, 3))
        parts = parts.reshape(EXPERTS * n_zl, group, width)
        outs = lax.all_to_all(parts, ("y", "zl"), split_axis=0, concat_axis=0, tiled=True)
        expert_cols = outs.reshape(EXPERTS * CAP, width).astype(jnp.float32)
        mixture = jnp.dot(combine[0], expert_cols, precision=lax.Precision.HIGHEST)
        layer_cols = (
            hidden_cols.astype(jnp.float32) + row_scale(mixture, col_slice(gain_post, width))
        ).astype(jnp.bfloat16)
        layer_out = lax.all_gather(layer_cols, CTX, axis=1, tiled=True)
    return layer_out[None]


def solution(mesh):
    n_exp = mesh.shape["exp"]
    n_ctx = mesh.shape["ctx"]
    sizes = {"y": EXPERTS, "x": n_exp // EXPERTS // 2, "zh": 2, "zl": n_ctx // 2, "core": 2}
    parts = {"exp": ("y", "x", "zh"), "ctx": ("zl", "core")}
    names = tuple(n for axis in mesh.axis_names for n in parts[axis])
    devices = np.asarray(mesh.devices).reshape(tuple(sizes[n] for n in names))
    fine = Mesh(devices, names)
    in_specs = (
        P(REQ, None, CTX),
        P(REQ, CTX, None),
        P(REQ, CTX, None),
        P(REQ, None, CTX),
        P(REQ, None, CTX),
        P(REQ, None),
        P(REQ, None, None),
        P(REQ, None, None),
        P(REQ, None, None),
        P(),
        P(),
        P(),
        P(REQ, None, CTX),
        P(REQ, None, CTX),
        P(REQ, CTX, None),
    )
    out_specs = P(REQ, None, None)
    return jax.shard_map(
        per_device, mesh=fine, in_specs=in_specs, out_specs=out_specs, check_vma=False
    )
```
